128 devices in a mesh: pair: 32 (over z, x, core), vgrp: 4 (over y).
Axes of the slice: x: 4, y: 4, z: 4, core: 2. Of those that a mesh axis runs over, the one named last changes fastest.
Arguments:
- amplitudes: bfloat16 [64, 768, 768], P('pair'), may hold values from -6 to 6
- cholesky_vectors: bfloat16 [4, 32, 768, 768], P('vgrp', 'pair'), may hold values from -0.21875 to 0.21875
- owner_order: int32 [4, 4], replicated, may hold values from 0 to 31, as said below
Outputs:
- residual: float32 [64, 768, 768], P('pair', 'vgrp')
The draws below stay inside these ranges and needn't reach their ends.
Inputs may be any that keep to these rules, and one draw needn't show every extreme that they name: `owner_order`: within one row the 4 entries are distinct; in every draw some row names both 0 and 31.
All inputs are finite; a program needn't handle non-finite values.
Results may differ from the reference program's by a relative error of at most 0.0029.
Values may be sent and summed in bfloat16 or wider, within the bound.
No kernel may reach another device: no remote copies, remote signals or barrier semaphores. Data moves between devices by JAX's collectives and lax.ppermute only.
A program may use at most 64 MiB of HBM per device.

```python
import jax
import jax.numpy as jnp
from jax import lax

V = 768
VECS = 4
PAIRS = 64
OWNERS = 32
GROUPS = 4


def draw_owner_order(key, part):
    keyring = jax.random.split(key, GROUPS + 1)
    chosen = jax.random.randint(keyring[0], (), 0, GROUPS)

    def one_group(subkey):
        key_drawn, key_inner, key_order = jax.random.split(subkey, 3)
        drawn = jax.random.permutation(key_drawn, OWNERS)[:VECS].astype(jnp.int32)
        inner = (jax.random.permutation(key_inner, OWNERS - 2)[:VECS - 2] + 1).astype(jnp.int32)
        ends = jnp.concatenate([jnp.array([0, OWNERS - 1], jnp.int32), inner])
        ends = ends[jax.random.permutation(key_order, VECS)]
        return (drawn, ends)
    plains, endings = jax.vmap(one_group)(keyring[1:])
    group_ids = jnp.arange(GROUPS, dtype=jnp.int32)[:, None]
    return jnp.where(group_ids == chosen, endings, plains).astype(jnp.int32)


def levels(key, extent, pieces, least, largest):
    loudness, own = 1.0, jax.random.fold_in(key, 6)
    for axis_at, blocks in pieces:
        draws = jnp.exp(jax.random.uniform(jax.random.fold_in(own, axis_at), (blocks,), jnp.float32, least / len(pieces), largest / len(pieces)))
        loudness = loudness * jnp.repeat(draws, extent[axis_at] // blocks).reshape([-1 if axis == axis_at else 1 for axis in range(len(extent))])
    return loudness


def noise(key, extent, deviation, limit, cuts=(), kind=jnp.bfloat16):
    result = deviation * jax.random.normal(key, extent, jnp.float32)
    if cuts:
        result = result * levels(key, extent, cuts, -0.22, 0.18)
    return jnp.clip(result, -limit, limit).astype(kind)


def setup_inputs(seed: int = 0) -> dict:
    keys = jax.random.split(jax.random.key(seed), 4)
    amplitudes = noise(keys[0], (PAIRS, V, V), 1.0, 6.0, ((0, 32),))
    cholesky_vectors = noise(keys[1], (GROUPS, OWNERS, V, V), V ** -0.5, 0.21875, ((0, 4), (1, 32)))
    owner_order = draw_owner_order(jax.random.fold_in(keys[3], 71), 0)
    return {"amplitudes": amplitudes, "cholesky_vectors": cholesky_vectors, "owner_order": owner_order}


def reference(amplitudes, cholesky_vectors, owner_order):
    group_rows = jnp.arange(GROUPS, dtype=jnp.int32)[:, None]
    selected = cholesky_vectors[group_rows, owner_order].reshape(GROUPS * VECS, V, V)

    def one_pair(amplitude):
        def add_vector(accumulated, vector):
            half_product = jnp.dot(vector, amplitude, preferred_element_type=jnp.float32).astype(jnp.bfloat16)
            return accumulated + jnp.dot(half_product, vector.T, preferred_element_type=jnp.float32), None

        accumulated, unused = lax.scan(add_vector, jnp.zeros((V, V), jnp.float32), selected)
        return accumulated

    return lax.map(one_pair, amplitudes)
```

```python
import jax
import jax.numpy as jnp
from jax import lax
from jax.sharding import Mesh
from jax.sharding import PartitionSpec as P

PAIR = ("z", "x", "core")
CHIPS = ("z", "x")


def gather_slots(own_vector, owned_slots):
    rows, cols = own_vector.shape
    devices = lax.psum(1, PAIR)
    cores = lax.psum(1, "core")
    piece = rows // devices
    pieces = own_vector.reshape(devices, piece, cols)
    pieces = lax.all_to_all(pieces, PAIR, 0, 0, tiled=True)
    picked = jnp.take(pieces, owned_slots, axis=0)
    mine = lax.all_gather(picked, CHIPS, axis=0, tiled=False)
    core = lax.axis_index("core")
    other = lax.ppermute(mine, "core", [(0, 1), (1, 0)])
    low = jnp.where(core == 0, mine, other)
    high = jnp.where(core == 0, other, mine)
    full = jnp.stack([low, high], axis=1)
    slots = owned_slots.shape[0]
    full = jnp.transpose(full, (2, 0, 1, 3, 4))
    return full.reshape(slots, rows, cols)


def on_device(amplitudes, cholesky_vectors, owner_order):
    vgrp_index = lax.axis_index("vgrp")
    owned_slots = lax.dynamic_index_in_dim(owner_order, vgrp_index, 0, keepdims=False)
    vectors = gather_slots(cholesky_vectors[0, 0], owned_slots)
    accumulated = jnp.zeros(amplitudes.shape, jnp.float32)
    for slot in range(owned_slots.shape[0]):
        vector = vectors[slot]
        half_product = jnp.einsum(
            "ac,pcd->pad", vector, amplitudes, preferred_element_type=jnp.float32
        ).astype(jnp.bfloat16)
        accumulated = accumulated + jnp.einsum(
            "pad,bd->pab", half_product, vector, preferred_element_type=jnp.float32
        )
    return lax.psum_scatter(accumulated, "vgrp", scatter_dimension=1, tiled=True)


def solution(mesh):
    pair, vgrp = mesh.devices.shape
    cores = 2
    chips = pair // cores
    side = int(round(chips ** 0.5))
    devices = mesh.devices.reshape(chips // side, side, cores, vgrp)
    fine = Mesh(devices, ("z", "x", "core", "vgrp"))
    placed = (P(PAIR, None, None), P("vgrp", PAIR, None, None), P())
    return jax.shard_map(
        on_device, mesh=fine, in_specs=placed, out_specs=P(PAIR, "vgrp", None), check_vma=False
    )
```

```python
import jax
import jax.numpy as jnp
from jax import lax
from jax.sharding import Mesh
from jax.sharding import PartitionSpec as P

PAIR = ("z", "x", "core")
CHIPS = ("z", "x")
RING = 4


def ring_axis(stage, core):
    return "x" if (stage == 1) == (core == 0) else "z"


def ring_perm(sizes, stage, step):
    nz, nx, nc = sizes
    perm = []
    for z in range(nz):
        for x in range(nx):
            for c in range(nc):
                if ring_axis(stage, c) == "x":
                    dz, dx = z, (x + step) % nx
                else:
                    dz, dx = (z + step) % nz, x
                perm.append(((z * nx + x) * nc + c, (dz * nx + dx) * nc + c))
    return perm


def ring_gather(piece, sizes, stage):
    half = piece.shape[0] // 2
    from_prev = lax.ppermute(piece, PAIR, ring_perm(sizes, stage, 1))
    from_next = lax.ppermute(piece, PAIR, ring_perm(sizes, stage, -1))
    far_low = lax.ppermute(from_prev[:half], PAIR, ring_perm(sizes, stage, 1))
    far_high = lax.ppermute(from_next[half:], PAIR, ring_perm(sizes, stage, -1))
    far = jnp.concatenate([far_low, far_high], axis=0)
    return jnp.stack([piece, from_next, far, from_prev], axis=0)


def gather_slots(own_vector, owned_slots, sizes):
    nz, nx, nc = sizes
    rows, cols = own_vector.shape
    devices = nz * nx * nc
    piece = rows // devices
    slots = owned_slots.shape[0]
    pieces = own_vector.reshape(devices, piece, cols)
    pieces = lax.all_to_all(pieces, PAIR, 0, 0, tiled=True)
    picked = jnp.take(pieces, owned_slots, axis=0)
    first = ring_gather(picked, sizes, 1)
    both = ring_gather(first, sizes, 2)
    swap = [(q, q ^ 1) for q in range(devices)]
    other = lax.ppermute(both, PAIR, swap)
    chips = nz * nx
    stacked = jnp.concatenate(
        [both.reshape((chips,) + both.shape[2:]), other.reshape((chips,) + both.shape[2:])], axis=0
    )
    z = lax.axis_index("z")
    x = lax.axis_index("x")
    core = lax.axis_index("core")
    q = jnp.arange(devices, dtype=jnp.int32)
    zq, xq, cq = q // (nx * nc), (q // nc) % nx, q % nc
    dz, dx = (zq - z) % nz, (xq - x) % nx
    inner = jnp.where(cq == 0, dz * nx + dx, dx * nz + dz)
    index = jnp.where(cq == core, 0, chips) + inner
    ordered = jnp.take(stacked, index, axis=0)
    ordered = jnp.transpose(ordered, (0, 2, 1, 3))
    return ordered.reshape(rows, slots, cols)


def on_device(amplitudes, cholesky_vectors, owner_order, sizes):
    vgrp = lax.axis_index("vgrp")
    groups = lax.psum(1, "vgrp")
    owned_slots = lax.dynamic_index_in_dim(owner_order, vgrp, 0, keepdims=False)
    vectors = gather_slots(cholesky_vectors[0, 0], owned_slots, sizes)
    rows, slots, cols = vectors.shape
    block = rows // groups
    flat = vectors.reshape(rows, slots * cols)

    def partial(pair, index):
        start = pl_multiple(index * block)
        mine = lax.dynamic_slice_in_dim(flat, start, block, axis=0)
        half = jnp.dot(
            mine.reshape(block * slots, cols), amplitudes[pair], preferred_element_type=jnp.float32
        ).astype(jnp.bfloat16)
        return lax.dot_general(
            half.reshape(block, slots * cols), flat, (((1,), (1,)), ((), ())),
            preferred_element_type=jnp.float32,
        )

    outs = []
    arrived = [None, None]
    directions = (1, -1)
    for step in range(RING):
        sums = []
        for pair, direction in enumerate(directions):
            index = (vgrp - direction * (1 + step)) % groups
            total = partial(pair, index)
            if arrived[pair] is not None:
                total = total + arrived[pair].astype(jnp.float32)
            sums.append(total)
        if step < RING - 1:
            for pair, direction in enumerate(directions):
                shift = [(g, (g + direction) % RING) for g in range(RING)]
                arrived[pair] = lax.ppermute(sums[pair].astype(jnp.bfloat16), "vgrp", shift)
        else:
            outs = sums
    return jnp.stack(outs, axis=0)


def pl_multiple(value):
    return value


def solution(mesh):
    pair, vgrp = mesh.devices.shape
    cores = 2
    chips = pair // cores
    side = RING
    assert chips == side * side and vgrp == RING
    devices = mesh.devices.reshape(chips // side, side, cores, vgrp)
    fine = Mesh(devices, ("z", "x", "core", "vgrp"))
    sizes = (chips // side, side, cores)
    placed = (P(PAIR, None, None), P("vgrp", PAIR, None, None), P())

    def body(amplitudes, cholesky_vectors, owner_order):
        return on_device(amplitudes, cholesky_vectors, owner_order, sizes)

    return jax.shard_map(
        body, mesh=fine, in_specs=placed, out_specs=P(PAIR, "vgrp", None), check_vma=False
    )
```

```python
import jax
import jax.numpy as jnp
from jax import lax
from jax.sharding import Mesh
from jax.sharding import PartitionSpec as P

PAIR = ("z", "x", "core")
CHIPS = ("z", "x")


def gather_slots(own_vector, owned_slots):
    rows, cols = own_vector.shape
    devices = lax.psum(1, PAIR)
    piece = rows // devices
    pieces = own_vector.reshape(devices, piece, cols)
    pieces = lax.all_to_all(pieces, PAIR, 0, 0, tiled=True)
    picked = jnp.take(pieces, owned_slots, axis=0)
    mine = lax.all_gather(picked, CHIPS, axis=0, tiled=False)
    core = lax.axis_index("core")
    other = lax.ppermute(mine, "core", [(0, 1), (1, 0)])
    low = jnp.where(core == 0, mine, other)
    high = jnp.where(core == 0, other, mine)
    full = jnp.stack([low, high], axis=1)
    slots = owned_slots.shape[0]
    full = jnp.transpose(full, (2, 0, 1, 3, 4))
    return full.reshape(slots, rows, cols)


def shifted(value, step, groups):
    return lax.ppermute(value, "vgrp", [(g, (g + step) % groups) for g in range(groups)])


def scatter_sum(total, vgrp, groups):
    rows, cols = total.shape
    block = rows // groups
    blocks = total.reshape(groups, block, cols)

    def pick(offset):
        return lax.dynamic_index_in_dim(blocks, (vgrp + offset) % groups, 0, keepdims=False)

    ahead = shifted(pick(1).astype(jnp.bfloat16), 1, groups)
    behind = shifted(pick(-1).astype(jnp.bfloat16), -1, groups)
    far = pick(2).astype(jnp.bfloat16)
    half = block // 2
    far_low = shifted(shifted(far[:half], 1, groups), 1, groups)
    far_high = shifted(shifted(far[half:], -1, groups), -1, groups)
    far = jnp.concatenate([far_low, far_high], axis=0)
    return pick(0) + ahead.astype(jnp.float32) + behind.astype(jnp.float32) + far.astype(jnp.float32)


def on_device(amplitudes, cholesky_vectors, owner_order):
    vgrp = lax.axis_index("vgrp")
    groups = lax.psum(1, "vgrp")
    owned_slots = lax.dynamic_index_in_dim(owner_order, vgrp, 0, keepdims=False)
    vectors = gather_slots(cholesky_vectors[0, 0], owned_slots)
    outs = []
    for pair in range(amplitudes.shape[0]):
        amplitude = amplitudes[pair]
        total = jnp.zeros(amplitude.shape, jnp.float32)
        for slot in range(owned_slots.shape[0]):
            vector = vectors[slot]
            half_product = jnp.dot(
                vector, amplitude, preferred_element_type=jnp.float32
            ).astype(jnp.bfloat16)
            total = total + lax.dot_general(
                half_product, vector, (((1,), (1,)), ((), ())), preferred_element_type=jnp.float32
            )
        outs.append(scatter_sum(total, vgrp, groups))
    return jnp.stack(outs, axis=0)


def solution(mesh):
    pair, vgrp = mesh.devices.shape
    cores = 2
    chips = pair // cores
    side = int(round(chips ** 0.5))
    devices = mesh.devices.reshape(chips // side, side, cores, vgrp)
    fine = Mesh(devices, ("z", "x", "core", "vgrp"))
    placed = (P(PAIR, None, None), P("vgrp", PAIR, None, None), P())
    return jax.shard_map(
        on_device, mesh=fine, in_specs=placed, out_specs=P(PAIR, "vgrp", None), check_vma=False
    )
```

```python
import jax
import jax.numpy as jnp
from jax import lax
from jax.sharding import Mesh
from jax.sharding import PartitionSpec as P

PAIR = ("z", "x", "core")
CHIPS = ("z", "x")


def gather_slots(own_vector, owned_slots):
    rows, cols = own_vector.shape
    devices = lax.psum(1, PAIR)
    piece = rows // devices
    pieces = own_vector.reshape(devices, piece, cols)
    pieces = lax.all_to_all(pieces, PAIR, 0, 0, tiled=True)
    picked = jnp.take(pieces, owned_slots, axis=0)
    mine = lax.all_gather(picked, CHIPS, axis=0, tiled=False)
    core = lax.axis_index("core")
    other = lax.ppermute(mine, "core", [(0, 1), (1, 0)])
    low = jnp.where(core == 0, mine, other)
    high = jnp.where(core == 0, other, mine)
    full = jnp.stack([low, high], axis=1)
    slots = owned_slots.shape[0]
    full = jnp.transpose(full, (2, 0, 1, 3, 4))
    return full.reshape(slots, rows, cols)


def shifted(value, step, groups):
    return lax.ppermute(value, "vgrp", [(g, (g + step) % groups) for g in range(groups)])


def scatter_sum(total, vgrp, groups):
    pairs, rows, cols = total.shape
    block = rows // groups
    half = block // 2
    blocks = total.reshape(pairs, groups, block, cols)

    def pick(offset):
        return lax.dynamic_index_in_dim(blocks, (vgrp + offset) % groups, 1, keepdims=False)

    far = pick(2).astype(jnp.bfloat16)
    ahead = jnp.concatenate([pick(1).astype(jnp.bfloat16), far[:, :half]], axis=1)
    behind = jnp.concatenate([pick(-1).astype(jnp.bfloat16), far[:, half:]], axis=1)
    ahead = shifted(ahead, 1, groups)
    behind = shifted(behind, -1, groups)
    far_low = shifted(ahead[:, block:], 1, groups)
    far_high = shifted(behind[:, block:], -1, groups)
    far = jnp.concatenate([far_low, far_high], axis=1).astype(jnp.float32)
    near = ahead[:, :block].astype(jnp.float32) + behind[:, :block].astype(jnp.float32)
    return pick(0) + near + far


def on_device(amplitudes, cholesky_vectors, owner_order):
    vgrp = lax.axis_index("vgrp")
    groups = lax.psum(1, "vgrp")
    owned_slots = lax.dynamic_index_in_dim(owner_order, vgrp, 0, keepdims=False)
    vectors = gather_slots(cholesky_vectors[0, 0], owned_slots)
    total = jnp.zeros(amplitudes.shape, jnp.float32)
    for slot in range(owned_slots.shape[0]):
        vector = vectors[slot]
        half_product = jnp.einsum(
            "ac,pcd->pad", vector, amplitudes, preferred_element_type=jnp.float32
        ).astype(jnp.bfloat16)
        total = total + jnp.einsum(
            "pad,bd->pab", half_product, vector, preferred_element_type=jnp.float32
        )
    return scatter_sum(total, vgrp, groups)


def solution(mesh):
    pair, vgrp = mesh.devices.shape
    cores = 2
    chips = pair // cores
    side = int(round(chips ** 0.5))
    devices = mesh.devices.reshape(chips // side, side, cores, vgrp)
    fine = Mesh(devices, ("z", "x", "core", "vgrp"))
    placed = (P(PAIR, None, None), P("vgrp", PAIR, None, None), P())
    return jax.shard_map(
        on_device, mesh=fine, in_specs=placed, out_specs=P(PAIR, "vgrp", None), check_vma=False
    )
```

```python
import jax
import jax.numpy as jnp
from jax import lax
from jax.sharding import Mesh
from jax.sharding import PartitionSpec as P

PAIR = ("z", "x", "core")
CHIPS = ("z", "x")


def gather_slots(own_vector, owned_slots):
    rows, cols = own_vector.shape
    devices = lax.psum(1, PAIR)
    piece = rows // devices
    pieces = own_vector.reshape(devices, piece, cols)
    pieces = lax.all_to_all(pieces, PAIR, 0, 0, tiled=True)
    picked = jnp.take(pieces, owned_slots, axis=0)
    mine = lax.all_gather(picked, CHIPS, axis=0, tiled=False)
    core = lax.axis_index("core")
    other = lax.ppermute(mine, "core", [(0, 1), (1, 0)])
    low = jnp.where(core == 0, mine, other)
    high = jnp.where(core == 0, other, mine)
    full = jnp.stack([low, high], axis=1)
    slots = owned_slots.shape[0]
    full = jnp.transpose(full, (2, 0, 1, 3, 4))
    return full.reshape(slots, rows, cols)


def shifted(value, step, groups):
    return lax.ppermute(value, "vgrp", [(g, (g + step) % groups) for g in range(groups)])


def on_device(amplitudes, cholesky_vectors, owner_order):
    vgrp = lax.axis_index("vgrp")
    groups = lax.psum(1, "vgrp")
    owned_slots = lax.dynamic_index_in_dim(owner_order, vgrp, 0, keepdims=False)
    vectors = gather_slots(cholesky_vectors[0, 0], owned_slots)
    slots, rows, cols = vectors.shape
    block = rows // groups
    half = block // 2

    def partial(offset):
        start = ((vgrp + offset) % groups) * block
        mine = lax.dynamic_slice_in_dim(vectors, start, block, axis=1)
        total = None
        for slot in range(slots):
            half_product = jnp.einsum(
                "ac,pcd->pad", mine[slot], amplitudes, preferred_element_type=jnp.float32
            ).astype(jnp.bfloat16)
            term = jnp.einsum(
                "pad,bd->pab", half_product, vectors[slot], preferred_element_type=jnp.float32
            )
            total = term if total is None else total + term
        return total

    far = partial(2).astype(jnp.bfloat16)
    far_low = shifted(far[:, :half], 1, groups)
    far_high = shifted(far[:, half:], -1, groups)
    far_low = shifted(far_low, 1, groups)
    far_high = shifted(far_high, -1, groups)
    ahead = shifted(partial(1).astype(jnp.bfloat16), 1, groups)
    behind = shifted(partial(-1).astype(jnp.bfloat16), -1, groups)
    own = partial(0)
    far = jnp.concatenate([far_low, far_high], axis=1).astype(jnp.float32)
    return own + ahead.astype(jnp.float32) + behind.astype(jnp.float32) + far


def solution(mesh):
    pair, vgrp = mesh.devices.shape
    cores = 2
    chips = pair // cores
    side = int(round(chips ** 0.5))
    devices = mesh.devices.reshape(chips // side, side, cores, vgrp)
    fine = Mesh(devices, ("z", "x", "core", "vgrp"))
    placed = (P(PAIR, None, None), P("vgrp", PAIR, None, None), P())
    return jax.shard_map(
        on_device, mesh=fine, in_specs=placed, out_specs=P(PAIR, "vgrp", None), check_vma=False
    )
```

```python
import jax
import jax.numpy as jnp
from jax import lax
from jax.sharding import Mesh
from jax.sharding import PartitionSpec as P

PAIR = ("z", "x", "core")
CHIPS = ("z", "x")


def gather_slots(own_vector, owned_slots):
    rows, cols = own_vector.shape
    devices = lax.psum(1, PAIR)
    piece = rows // devices
    pieces = own_vector.reshape(devices, piece, cols)
    pieces = lax.all_to_all(pieces, PAIR, 0, 0, tiled=True)
    picked = jnp.take(pieces, owned_slots, axis=0)
    mine = lax.all_gather(picked, CHIPS, axis=0, tiled=False)
    core = lax.axis_index("core")
    other = lax.ppermute(mine, "core", [(0, 1), (1, 0)])
    low = jnp.where(core == 0, mine, other)
    high = jnp.where(core == 0, other, mine)
    full = jnp.stack([low, high], axis=1)
    slots = owned_slots.shape[0]
    full = jnp.transpose(full, (2, 0, 1, 3, 4))
    return full.reshape(slots, rows, cols)


def shifted(value, step, groups):
    return lax.ppermute(value, "vgrp", [(g, (g + step) % groups) for g in range(groups)])


def scatter_sum(total, vgrp, groups):
    pairs, rows, cols = total.shape
    block = rows // groups
    blocks = total.reshape(pairs, groups, block, cols)

    def pick(offset):
        return lax.dynamic_index_in_dim(blocks, (vgrp + offset) % groups, 1, keepdims=False)

    ahead = shifted(pick(1).astype(jnp.bfloat16), 1, groups)
    behind = shifted(pick(-1).astype(jnp.bfloat16), -1, groups)
    far = shifted(pick(2).astype(jnp.bfloat16), 2, groups)
    near = ahead.astype(jnp.float32) + behind.astype(jnp.float32)
    return pick(0) + near + far.astype(jnp.float32)


def on_device(amplitudes, cholesky_vectors, owner_order):
    vgrp = lax.axis_index("vgrp")
    groups = lax.psum(1, "vgrp")
    owned_slots = lax.dynamic_index_in_dim(owner_order, vgrp, 0, keepdims=False)
    vectors = gather_slots(cholesky_vectors[0, 0], owned_slots)
    total = jnp.zeros(amplitudes.shape, jnp.float32)
    for slot in range(owned_slots.shape[0]):
        vector = vectors[slot]
        half_product = jnp.einsum(
            "ac,pcd->pad", vector, amplitudes, preferred_element_type=jnp.float32
        ).astype(jnp.bfloat16)
        total = total + jnp.einsum(
            "pad,bd->pab", half_product, vector, preferred_element_type=jnp.float32
        )
    return scatter_sum(total, vgrp, groups)


def solution(mesh):
    pair, vgrp = mesh.devices.shape
    cores = 2
    chips = pair // cores
    side = int(round(chips ** 0.5))
    devices = mesh.devices.reshape(chips // side, side, cores, vgrp)
    fine = Mesh(devices, ("z", "x", "core", "vgrp"))
    placed = (P(PAIR, None, None), P("vgrp", PAIR, None, None), P())
    return jax.shard_map(
        on_device, mesh=fine, in_specs=placed, out_specs=P(PAIR, "vgrp", None), check_vma=False
    )
```

```python
import jax
import jax.numpy as jnp
from jax import lax
from jax.sharding import Mesh
from jax.sharding import PartitionSpec as P

PAIR = ("z", "x", "core")
CHIPS = ("z", "x")


RING = 4


def ring_axis(stage, core):
    return "x" if (stage == 1) == (core == 0) else "z"


def ring_perm(sizes, stage, step):
    nz, nx, nc = sizes
    perm = []
    for z in range(nz):
        for x in range(nx):
            for c in range(nc):
                if ring_axis(stage, c) == "x":
                    dz, dx = z, (x + step) % nx
                else:
                    dz, dx = (z + step) % nz, x
                perm.append(((z * nx + x) * nc + c, (dz * nx + dx) * nc + c))
    return perm


def ring_gather(piece, sizes, stage):
    half = piece.shape[0] // 2
    from_prev = lax.ppermute(piece, PAIR, ring_perm(sizes, stage, 1))
    from_next = lax.ppermute(piece, PAIR, ring_perm(sizes, stage, -1))
    far_low = lax.ppermute(from_prev[:half], PAIR, ring_perm(sizes, stage, 1))
    far_high = lax.ppermute(from_next[half:], PAIR, ring_perm(sizes, stage, -1))
    far = jnp.concatenate([far_low, far_high], axis=0)
    return jnp.stack([piece, from_next, far, from_prev], axis=0)


def gather_slots(own_vector, owned_slots, sizes):
    nz, nx, nc = sizes
    rows, cols = own_vector.shape
    devices = nz * nx * nc
    piece = rows // devices
    slots = owned_slots.shape[0]
    pieces = own_vector.reshape(devices, piece, cols)
    pieces = lax.all_to_all(pieces, PAIR, 0, 0, tiled=True)
    picked = jnp.take(pieces, owned_slots, axis=0)
    first = ring_gather(picked, sizes, 1)
    both = ring_gather(first, sizes, 2)
    swap = [(q, q ^ 1) for q in range(devices)]
    other = lax.ppermute(both, PAIR, swap)
    chips = nz * nx
    stacked = jnp.concatenate(
        [both.reshape((chips,) + both.shape[2:]), other.reshape((chips,) + both.shape[2:])], axis=0
    )
    z = lax.axis_index("z")
    x = lax.axis_index("x")
    core = lax.axis_index("core")
    q = jnp.arange(devices, dtype=jnp.int32)
    zq, xq, cq = q // (nx * nc), (q // nc) % nx, q % nc
    dz, dx = (zq - z) % nz, (xq - x) % nx
    inner = jnp.where(cq == 0, dz * nx + dx, dx * nz + dz)
    index = jnp.where(cq == core, 0, chips) + inner
    ordered = jnp.take(stacked, index, axis=0)
    ordered = jnp.transpose(ordered, (1, 0, 2, 3))
    return ordered.reshape(slots, rows, cols)


def shifted(value, step, groups):
    return lax.ppermute(value, "vgrp", [(g, (g + step) % groups) for g in range(groups)])


def scatter_sum(total, vgrp, groups):
    pairs, rows, cols = total.shape
    block = rows // groups
    blocks = total.reshape(pairs, groups, block, cols)

    def pick(offset):
        return lax.dynamic_index_in_dim(blocks, (vgrp + offset) % groups, 1, keepdims=False)

    ahead = shifted(pick(1).astype(jnp.bfloat16), 1, groups)
    behind = shifted(pick(-1).astype(jnp.bfloat16), -1, groups)
    far = shifted(pick(2).astype(jnp.bfloat16), 2, groups)
    near = ahead.astype(jnp.float32) + behind.astype(jnp.float32)
    return pick(0) + near + far.astype(jnp.float32)


def on_device(amplitudes, cholesky_vectors, owner_order, sizes):
    vgrp = lax.axis_index("vgrp")
    groups = lax.psum(1, "vgrp")
    owned_slots = lax.dynamic_index_in_dim(owner_order, vgrp, 0, keepdims=False)
    vectors = gather_slots(cholesky_vectors[0, 0], owned_slots, sizes)
    total = jnp.zeros(amplitudes.shape, jnp.float32)
    for slot in range(owned_slots.shape[0]):
        vector = vectors[slot]
        half_product = jnp.einsum(
            "ac,pcd->pad", vector, amplitudes, preferred_element_type=jnp.float32
        ).astype(jnp.bfloat16)
        total = total + jnp.einsum(
            "pad,bd->pab", half_product, vector, preferred_element_type=jnp.float32
        )
    return scatter_sum(total, vgrp, groups)


def solution(mesh):
    pair, vgrp = mesh.devices.shape
    cores = 2
    chips = pair // cores
    side = RING
    assert chips == side * side
    devices = mesh.devices.reshape(chips // side, side, cores, vgrp)
    fine = Mesh(devices, ("z", "x", "core", "vgrp"))
    sizes = (chips // side, side, cores)
    placed = (P(PAIR, None, None), P("vgrp", PAIR, None, None), P())

    def body(amplitudes, cholesky_vectors, owner_order):
        return on_device(amplitudes, cholesky_vectors, owner_order, sizes)

    return jax.shard_map(
        body, mesh=fine, in_specs=placed, out_specs=P(PAIR, "vgrp", None), check_vma=False
    )
```

```python
import jax
import jax.numpy as jnp
from jax import lax
from jax.sharding import Mesh
from jax.sharding import PartitionSpec as P

PAIR = ("z", "x", "core")
CHIPS = ("z", "x")


RING = 4


def ring_axis(stage, core):
    return "x" if (stage == 1) == (core == 0) else "z"


def ring_perm(sizes, stage, step):
    nz, nx, nc = sizes
    perm = []
    for z in range(nz):
        for x in range(nx):
            for c in range(nc):
                if ring_axis(stage, c) == "x":
                    dz, dx = z, (x + step) % nx
                else:
                    dz, dx = (z + step) % nz, x
                perm.append(((z * nx + x) * nc + c, (dz * nx + dx) * nc + c))
    return perm


def ring_gather(piece, sizes, stage, direct_far=False):
    half = piece.shape[0] // 2
    from_prev = lax.ppermute(piece, PAIR, ring_perm(sizes, stage, 1))
    from_next = lax.ppermute(piece, PAIR, ring_perm(sizes, stage, -1))
    if direct_far:
        far = lax.ppermute(piece, PAIR, ring_perm(sizes, stage, 2))
    else:
        far_low = lax.ppermute(from_prev[:half], PAIR, ring_perm(sizes, stage, 1))
        far_high = lax.ppermute(from_next[half:], PAIR, ring_perm(sizes, stage, -1))
        far = jnp.concatenate([far_low, far_high], axis=0)
    return jnp.stack([piece, from_next, far, from_prev], axis=0)


def gather_slots(own_vector, owned_slots, sizes):
    nz, nx, nc = sizes
    rows, cols = own_vector.shape
    devices = nz * nx * nc
    piece = rows // devices
    slots = owned_slots.shape[0]
    pieces = own_vector.reshape(devices, piece, cols)
    pieces = lax.all_to_all(pieces, PAIR, 0, 0, tiled=True)
    picked = jnp.take(pieces, owned_slots, axis=0)
    first = ring_gather(picked, sizes, 1, direct_far=True)
    both = ring_gather(first, sizes, 2)
    swap = [(q, q ^ 1) for q in range(devices)]
    other = lax.ppermute(both, PAIR, swap)
    chips = nz * nx
    z = lax.axis_index("z")
    x = lax.axis_index("x")
    core = lax.axis_index("core")
    chip = jnp.arange(chips, dtype=jnp.int32)
    dz, dx = (chip // nx - z) % nz, (chip % nx - x) % nx
    x_first = dz * nx + dx
    z_first = dx * nz + dz
    mine = both.reshape((chips,) + both.shape[2:])
    other = other.reshape((chips,) + both.shape[2:])
    mine = jnp.take(mine, jnp.where(core == 0, x_first, z_first), axis=0)
    other = jnp.take(other, jnp.where(core == 0, z_first, x_first), axis=0)
    low = jnp.where(core == 0, mine, other)
    high = jnp.where(core == 0, other, mine)
    ordered = jnp.stack([low, high], axis=1)
    ordered = jnp.transpose(ordered, (2, 0, 1, 3, 4))
    return ordered.reshape(slots, rows, cols)


def shifted(value, step, groups):
    return lax.ppermute(value, "vgrp", [(g, (g + step) % groups) for g in range(groups)])


def scatter_sum(total, vgrp, groups):
    pairs, rows, cols = total.shape
    block = rows // groups
    blocks = total.reshape(pairs, groups, block, cols)

    def pick(offset):
        return lax.dynamic_index_in_dim(blocks, (vgrp + offset) % groups, 1, keepdims=False)

    ahead = shifted(pick(1).astype(jnp.bfloat16), 1, groups)
    behind = shifted(pick(-1).astype(jnp.bfloat16), -1, groups)
    far = pick(2).astype(jnp.bfloat16)
    half = block // 2
    far_low = shifted(far[:, :half], 2, groups)
    far_high = shifted(shifted(far[:, half:], 1, groups), 1, groups)
    far = jnp.concatenate([far_low, far_high], axis=1)
    near = ahead.astype(jnp.float32) + behind.astype(jnp.float32)
    return pick(0) + near + far.astype(jnp.float32)


def on_device(amplitudes, cholesky_vectors, owner_order, sizes):
    vgrp = lax.axis_index("vgrp")
    groups = lax.psum(1, "vgrp")
    owned_slots = lax.dynamic_index_in_dim(owner_order, vgrp, 0, keepdims=False)
    vectors = gather_slots(cholesky_vectors[0, 0], owned_slots, sizes)
    total = jnp.zeros(amplitudes.shape, jnp.float32)
    for slot in range(owned_slots.shape[0]):
        vector = vectors[slot]
        half_product = jnp.einsum(
            "ac,pcd->pad", vector, amplitudes, preferred_element_type=jnp.float32
        ).astype(jnp.bfloat16)
        total = total + jnp.einsum(
            "pad,bd->pab", half_product, vector, preferred_element_type=jnp.float32
        )
    return scatter_sum(total, vgrp, groups)


def solution(mesh):
    pair, vgrp = mesh.devices.shape
    cores = 2
    chips = pair // cores
    side = RING
    assert chips == side * side
    devices = mesh.devices.reshape(chips // side, side, cores, vgrp)
    fine = Mesh(devices, ("z", "x", "core", "vgrp"))
    sizes = (chips // side, side, cores)
    placed = (P(PAIR, None, None), P("vgrp", PAIR, None, None), P())

    def body(amplitudes, cholesky_vectors, owner_order):
        return on_device(amplitudes, cholesky_vectors, owner_order, sizes)

    return jax.shard_map(
        body, mesh=fine, in_specs=placed, out_specs=P(PAIR, "vgrp", None), check_vma=False
    )
```

```python
import jax
import jax.numpy as jnp
from jax import lax
from jax.sharding import Mesh
from jax.sharding import PartitionSpec as P

PAIR = ("z", "x", "core")
CHIPS = ("z", "x")


RING = 4


def ring_axis(stage, core):
    return "x" if (stage == 1) == (core == 0) else "z"


def ring_perm(sizes, stage, step):
    nz, nx, nc = sizes
    perm = []
    for z in range(nz):
        for x in range(nx):
            for c in range(nc):
                if ring_axis(stage, c) == "x":
                    dz, dx = z, (x + step) % nx
                else:
                    dz, dx = (z + step) % nz, x
                perm.append(((z * nx + x) * nc + c, (dz * nx + dx) * nc + c))
    return perm


def ring_gather(piece, sizes, stage, direct_far=False):
    half = piece.shape[0] // 2
    from_prev = lax.ppermute(piece, PAIR, ring_perm(sizes, stage, 1))
    from_next = lax.ppermute(piece, PAIR, ring_perm(sizes, stage, -1))
    if direct_far:
        far = lax.ppermute(piece, PAIR, ring_perm(sizes, stage, 2))
    else:
        far_low = lax.ppermute(from_prev[:half], PAIR, ring_perm(sizes, stage, 1))
        far_high = lax.ppermute(from_next[half:], PAIR, ring_perm(sizes, stage, -1))
        far = jnp.concatenate([far_low, far_high], axis=0)
    return jnp.stack([piece, from_next, far, from_prev], axis=0)


def gather_slots(own_vector, owned_slots, sizes):
    nz, nx, nc = sizes
    rows, cols = own_vector.shape
    devices = nz * nx * nc
    piece = rows // devices
    slots = owned_slots.shape[0]
    pieces = own_vector.reshape(devices, piece, cols)
    pieces = lax.all_to_all(pieces, PAIR, 0, 0, tiled=True)
    picked = jnp.take(pieces, owned_slots, axis=0)
    first = ring_gather(picked, sizes, 1, direct_far=True)
    both = ring_gather(first, sizes, 2)
    swap = [(q, q ^ 1) for q in range(devices)]
    other = lax.ppermute(both, PAIR, swap)
    chips = nz * nx
    stacked = jnp.concatenate(
        [both.reshape((chips,) + both.shape[2:]), other.reshape((chips,) + both.shape[2:])], axis=0
    )
    z = lax.axis_index("z")
    x = lax.axis_index("x")
    core = lax.axis_index("core")
    q = jnp.arange(devices, dtype=jnp.int32)
    zq, xq, cq = q // (nx * nc), (q // nc) % nx, q % nc
    dz, dx = (zq - z) % nz, (xq - x) % nx
    inner = jnp.where(cq == 0, dz * nx + dx, dx * nz + dz)
    index = jnp.where(cq == core, 0, chips) + inner
    ordered = jnp.take(stacked, index, axis=0)
    ordered = jnp.transpose(ordered, (1, 0, 2, 3))
    return ordered.reshape(slots, rows, cols)


def shifted(value, step, groups):
    return lax.ppermute(value, "vgrp", [(g, (g + step) % groups) for g in range(groups)])


def scatter_sum(total, vgrp, groups):
    pairs, rows, cols = total.shape
    block = rows // groups
    blocks = total.reshape(pairs, groups, block, cols)

    def pick(offset):
        return lax.dynamic_index_in_dim(blocks, (vgrp + offset) % groups, 1, keepdims=False)

    ahead = shifted(pick(1).astype(jnp.bfloat16), 1, groups)
    behind = shifted(pick(-1).astype(jnp.bfloat16), -1, groups)
    far = shifted(pick(2).astype(jnp.bfloat16), 2, groups)
    near = ahead.astype(jnp.float32) + behind.astype(jnp.float32)
    return pick(0) + near + far.astype(jnp.float32)


def on_device(amplitudes, cholesky_vectors, owner_order, sizes):
    vgrp = lax.axis_index("vgrp")
    groups = lax.psum(1, "vgrp")
    owned_slots = lax.dynamic_index_in_dim(owner_order, vgrp, 0, keepdims=False)
    vectors = gather_slots(cholesky_vectors[0, 0], owned_slots, sizes)
    total = jnp.zeros(amplitudes.shape, jnp.float32)
    for slot in range(owned_slots.shape[0]):
        vector = vectors[slot]
        half_product = jnp.einsum(
            "ac,pcd->pad", vector, amplitudes, preferred_element_type=jnp.float32
        ).astype(jnp.bfloat16)
        total = total + jnp.einsum(
            "pad,bd->pab", half_product, vector, preferred_element_type=jnp.float32
        )
    return scatter_sum(total, vgrp, groups)


def solution(mesh):
    pair, vgrp = mesh.devices.shape
    cores = 2
    chips = pair // cores
    side = RING
    assert chips == side * side
    devices = mesh.devices.reshape(chips // side, side, cores, vgrp)
    fine = Mesh(devices, ("z", "x", "core", "vgrp"))
    sizes = (chips // side, side, cores)
    placed = (P(PAIR, None, None), P("vgrp", PAIR, None, None), P())

    def body(amplitudes, cholesky_vectors, owner_order):
        return on_device(amplitudes, cholesky_vectors, owner_order, sizes)

    return jax.shard_map(
        body, mesh=fine, in_specs=placed, out_specs=P(PAIR, "vgrp", None), check_vma=False
    )
```

```python
import jax
import jax.numpy as jnp
from jax import lax
from jax.sharding import Mesh
from jax.sharding import PartitionSpec as P


PAIR = ("z", "x", "core")


RING = 4


def ring_axis(stage, core):
    return "x" if (stage == 1) == (core == 0) else "z"


def ring_perm(sizes, stage, step):
    nz, nx, nc = sizes
    perm = []
    for z in range(nz):
        for x in range(nx):
            for c in range(nc):
                if ring_axis(stage, c) == "x":
                    dz, dx = z, (x + step) % nx
                else:
                    dz, dx = (z + step) % nz, x
                perm.append(((z * nx + x) * nc + c, (dz * nx + dx) * nc + c))
    return perm


def ring_gather(piece, sizes, stage, direct_far=False):
    half = piece.shape[0] // 2
    from_prev = lax.ppermute(piece, PAIR, ring_perm(sizes, stage, 1))
    from_next = lax.ppermute(piece, PAIR, ring_perm(sizes, stage, -1))
    if direct_far:
        far = lax.ppermute(piece, PAIR, ring_perm(sizes, stage, 2))
    else:
        far_low = lax.ppermute(from_prev[:half], PAIR, ring_perm(sizes, stage, 1))
        far_high = lax.ppermute(from_next[half:], PAIR, ring_perm(sizes, stage, -1))
        far = jnp.concatenate([far_low, far_high], axis=0)
    return jnp.stack([piece, from_next, far, from_prev], axis=0)


def gather_slots(own_vector, owned_slots, sizes):
    nz, nx, nc = sizes
    rows, cols = own_vector.shape
    devices = nz * nx * nc
    piece = rows // devices
    slots = owned_slots.shape[0]
    pieces = own_vector.reshape(devices, piece, cols)
    pieces = lax.all_to_all(pieces, PAIR, 0, 0, tiled=True)
    picked = jnp.take(pieces, owned_slots, axis=0)
    first = ring_gather(picked, sizes, 1, direct_far=True)
    both = ring_gather(first, sizes, 2)
    swap = [(q, q ^ 1) for q in range(devices)]
    other = lax.ppermute(both, PAIR, swap)
    chips = nz * nx
    stacked = jnp.concatenate(
        [both.reshape((chips,) + both.shape[2:]), other.reshape((chips,) + both.shape[2:])], axis=0
    )
    z = lax.axis_index("z")
    x = lax.axis_index("x")
    core = lax.axis_index("core")
    q = jnp.arange(devices, dtype=jnp.int32)
    zq, xq, cq = q // (nx * nc), (q // nc) % nx, q % nc
    dz, dx = (zq - z) % nz, (xq - x) % nx
    inner = jnp.where(cq == 0, dz * nx + dx, dx * nz + dz)
    index = jnp.where(cq == core, 0, chips) + inner
    ordered = jnp.take(stacked, index, axis=0)
    ordered = jnp.transpose(ordered, (1, 0, 2, 3))
    return ordered.reshape(slots, rows, cols)


def shifted(value, step, groups):
    return lax.ppermute(value, "vgrp", [(g, (g + step) % groups) for g in range(groups)])


def prepare(total, vgrp, groups):
    pairs, rows, cols = total.shape
    block = rows // groups
    blocks = total.reshape(pairs, groups, block, cols)

    def pick(offset):
        return lax.dynamic_index_in_dim(blocks, (vgrp + offset) % groups, 1, keepdims=False)

    owed = tuple(pick(offset).astype(jnp.bfloat16) for offset in (1, -1, 2))
    return pick(0), owed


def exchange(own, owed, groups):
    ahead, behind, far = owed
    half = far.shape[1] // 2
    ahead = shifted(ahead, 1, groups)
    behind = shifted(behind, -1, groups)
    far_low = shifted(far[:, :half], 2, groups)
    far_high = shifted(far[:, half:], 1, groups)
    far_high = shifted(far_high, 1, groups)
    far = jnp.concatenate([far_low, far_high], axis=1)
    near = ahead.astype(jnp.float32) + behind.astype(jnp.float32)
    return own + near + far.astype(jnp.float32)


def columns(halves, vectors, lo, hi):
    total = None
    for slot, half_product in enumerate(halves):
        term = jnp.einsum(
            "pad,bd->pab", half_product, vectors[slot, lo:hi], preferred_element_type=jnp.float32
        )
        total = term if total is None else total + term
    return total


def on_device(amplitudes, cholesky_vectors, owner_order, sizes):
    vgrp = lax.axis_index("vgrp")
    groups = lax.psum(1, "vgrp")
    owned_slots = lax.dynamic_index_in_dim(owner_order, vgrp, 0, keepdims=False)
    vectors = gather_slots(cholesky_vectors[0, 0], owned_slots, sizes)
    halves = tuple(
        jnp.einsum(
            "ac,pcd->pad", vectors[slot], amplitudes, preferred_element_type=jnp.float32
        ).astype(jnp.bfloat16)
        for slot in range(vectors.shape[0])
    )
    split = vectors.shape[1] // 2
    own_a, owed_a = prepare(columns(halves, vectors, 0, split), vgrp, groups)
    halves, owed_a = lax.optimization_barrier((halves, owed_a))
    out_a = exchange(own_a, owed_a, groups)
    own_b, owed_b = prepare(columns(halves, vectors, split, None), vgrp, groups)
    out_b = exchange(own_b, owed_b, groups)
    return jnp.concatenate([out_a, out_b], axis=2)


def solution(mesh):
    pair, vgrp = mesh.devices.shape
    cores = 2
    chips = pair // cores
    side = RING
    assert chips == side * side
    devices = mesh.devices.reshape(chips // side, side, cores, vgrp)
    fine = Mesh(devices, ("z", "x", "core", "vgrp"))
    sizes = (chips // side, side, cores)
    placed = (P(PAIR, None, None), P("vgrp", PAIR, None, None), P())

    def body(amplitudes, cholesky_vectors, owner_order):
        return on_device(amplitudes, cholesky_vectors, owner_order, sizes)

    return jax.shard_map(
        body, mesh=fine, in_specs=placed, out_specs=P(PAIR, "vgrp", None), check_vma=False
    )
```

```python
import jax
import jax.numpy as jnp
from jax import lax
from jax.sharding import Mesh
from jax.sharding import PartitionSpec as P


PAIR = ("z", "x", "core")


RING = 4


def ring_axis(stage, core):
    return "x" if (stage == 1) == (core == 0) else "z"


def ring_perm(sizes, stage, step):
    nz, nx, nc = sizes
    perm = []
    for z in range(nz):
        for x in range(nx):
            for c in range(nc):
                if ring_axis(stage, c) == "x":
                    dz, dx = z, (x + step) % nx
                else:
                    dz, dx = (z + step) % nz, x
                perm.append(((z * nx + x) * nc + c, (dz * nx + dx) * nc + c))
    return perm


def ring_gather(piece, sizes, stage, direct_far=False):
    half = piece.shape[0] // 2
    from_prev = lax.ppermute(piece, PAIR, ring_perm(sizes, stage, 1))
    from_next = lax.ppermute(piece, PAIR, ring_perm(sizes, stage, -1))
    if direct_far:
        far = lax.ppermute(piece, PAIR, ring_perm(sizes, stage, 2))
    else:
        far_low = lax.ppermute(from_prev[:half], PAIR, ring_perm(sizes, stage, 1))
        far_high = lax.ppermute(from_next[half:], PAIR, ring_perm(sizes, stage, -1))
        far = jnp.concatenate([far_low, far_high], axis=0)
    return jnp.stack([piece, from_next, far, from_prev], axis=0)


def gather_slots(own_vector, owned_slots, sizes):
    nz, nx, nc = sizes
    rows, cols = own_vector.shape
    devices = nz * nx * nc
    piece = rows // devices
    slots = owned_slots.shape[0]
    pieces = own_vector.reshape(devices, piece, cols)
    pieces = lax.all_to_all(pieces, PAIR, 0, 0, tiled=True)
    picked = jnp.take(pieces, owned_slots, axis=0)
    first = ring_gather(picked, sizes, 1, direct_far=True)
    both = ring_gather(first, sizes, 2)
    swap = [(q, q ^ 1) for q in range(devices)]
    other = lax.ppermute(both, PAIR, swap)
    chips = nz * nx
    stacked = jnp.concatenate(
        [both.reshape((chips,) + both.shape[2:]), other.reshape((chips,) + both.shape[2:])], axis=0
    )
    z = lax.axis_index("z")
    x = lax.axis_index("x")
    core = lax.axis_index("core")
    q = jnp.arange(devices, dtype=jnp.int32)
    zq, xq, cq = q // (nx * nc), (q // nc) % nx, q % nc
    dz, dx = (zq - z) % nz, (xq - x) % nx
    inner = jnp.where(cq == 0, dz * nx + dx, dx * nz + dz)
    index = jnp.where(cq == core, 0, chips) + inner
    ordered = jnp.take(stacked, index, axis=0)
    ordered = jnp.transpose(ordered, (1, 0, 2, 3))
    return ordered.reshape(slots, rows, cols)


def shifted(value, step, groups):
    return lax.ppermute(value, "vgrp", [(g, (g + step) % groups) for g in range(groups)])


def prepare(total, vgrp, groups):
    pairs, rows, cols = total.shape
    block = rows // groups
    blocks = total.reshape(pairs, groups, block, cols)

    def pick(offset):
        return lax.dynamic_index_in_dim(blocks, (vgrp + offset) % groups, 1, keepdims=False)

    return pick(0), (pick(1), pick(-1), pick(2).astype(jnp.bfloat16))


def exchange(own, owed, groups):
    ahead, behind, far = owed
    half = far.shape[1] // 2
    far_up = shifted(far[:, :half], 1, groups)
    far_down = shifted(far[:, half:], -1, groups)
    ahead = jnp.concatenate([ahead[:, :half] + far_up.astype(jnp.float32), ahead[:, half:]], axis=1)
    behind = jnp.concatenate([behind[:, :half], behind[:, half:] + far_down.astype(jnp.float32)], axis=1)
    ahead = shifted(ahead.astype(jnp.bfloat16), 1, groups)
    behind = shifted(behind.astype(jnp.bfloat16), -1, groups)
    return own + ahead.astype(jnp.float32) + behind.astype(jnp.float32)


def columns(halves, vectors, lo, hi):
    total = None
    for slot, half_product in enumerate(halves):
        term = jnp.einsum(
            "pad,bd->pab", half_product, vectors[slot, lo:hi], preferred_element_type=jnp.float32
        )
        total = term if total is None else total + term
    return total


def on_device(amplitudes, cholesky_vectors, owner_order, sizes):
    vgrp = lax.axis_index("vgrp")
    groups = lax.psum(1, "vgrp")
    owned_slots = lax.dynamic_index_in_dim(owner_order, vgrp, 0, keepdims=False)
    vectors = gather_slots(cholesky_vectors[0, 0], owned_slots, sizes)
    halves = tuple(
        jnp.einsum(
            "ac,pcd->pad", vectors[slot], amplitudes, preferred_element_type=jnp.float32
        ).astype(jnp.bfloat16)
        for slot in range(vectors.shape[0])
    )
    split = vectors.shape[1] // 2
    own_a, owed_a = prepare(columns(halves, vectors, 0, split), vgrp, groups)
    halves, owed_a = lax.optimization_barrier((halves, owed_a))
    out_a = exchange(own_a, owed_a, groups)
    own_b, owed_b = prepare(columns(halves, vectors, split, None), vgrp, groups)
    out_b = exchange(own_b, owed_b, groups)
    return jnp.concatenate([out_a, out_b], axis=2)


def solution(mesh):
    pair, vgrp = mesh.devices.shape
    cores = 2
    chips = pair // cores
    side = RING
    assert chips == side * side
    devices = mesh.devices.reshape(chips // side, side, cores, vgrp)
    fine = Mesh(devices, ("z", "x", "core", "vgrp"))
    sizes = (chips // side, side, cores)
    placed = (P(PAIR, None, None), P("vgrp", PAIR, None, None), P())

    def body(amplitudes, cholesky_vectors, owner_order):
        return on_device(amplitudes, cholesky_vectors, owner_order, sizes)

    return jax.shard_map(
        body, mesh=fine, in_specs=placed, out_specs=P(PAIR, "vgrp", None), check_vma=False
    )
```

```python
import jax
import jax.numpy as jnp
from jax import lax
from jax.sharding import Mesh
from jax.sharding import PartitionSpec as P


PAIR = ("z", "x", "core")


RING = 4


def ring_axis(stage, core):
    return "x" if (stage == 1) == (core == 0) else "z"


def ring_perm(sizes, stage, step):
    nz, nx, nc = sizes
    perm = []
    for z in range(nz):
        for x in range(nx):
            for c in range(nc):
                if ring_axis(stage, c) == "x":
                    dz, dx = z, (x + step) % nx
                else:
                    dz, dx = (z + step) % nz, x
                perm.append(((z * nx + x) * nc + c, (dz * nx + dx) * nc + c))
    return perm


def ring_gather(piece, sizes, stage, direct_far=False):
    half = piece.shape[0] // 2
    from_prev = lax.ppermute(piece, PAIR, ring_perm(sizes, stage, 1))
    from_next = lax.ppermute(piece, PAIR, ring_perm(sizes, stage, -1))
    if direct_far:
        far = lax.ppermute(piece, PAIR, ring_perm(sizes, stage, 2))
    else:
        far_low = lax.ppermute(from_prev[:half], PAIR, ring_perm(sizes, stage, 1))
        far_high = lax.ppermute(from_next[half:], PAIR, ring_perm(sizes, stage, -1))
        far = jnp.concatenate([far_low, far_high], axis=0)
    return jnp.stack([piece, from_next, far, from_prev], axis=0)


def gather_slots(own_vector, owned_slots, sizes):
    nz, nx, nc = sizes
    rows, cols = own_vector.shape
    devices = nz * nx * nc
    piece = rows // devices
    slots = owned_slots.shape[0]
    pieces = own_vector.reshape(devices, piece, cols)
    pieces = lax.all_to_all(pieces, PAIR, 0, 0, tiled=True)
    picked = pieces.at[owned_slots].get(mode="promise_in_bounds")
    first = ring_gather(picked, sizes, 1, direct_far=True)
    both = ring_gather(first, sizes, 2)
    swap = [(q, q ^ 1) for q in range(devices)]
    other = lax.ppermute(both, PAIR, swap)
    chips = nz * nx
    stacked = jnp.concatenate(
        [both.reshape((chips,) + both.shape[2:]), other.reshape((chips,) + both.shape[2:])], axis=0
    )
    z = lax.axis_index("z")
    x = lax.axis_index("x")
    core = lax.axis_index("core")
    q = jnp.arange(devices, dtype=jnp.int32)
    zq, xq, cq = q // (nx * nc), (q // nc) % nx, q % nc
    dz, dx = (zq - z) % nz, (xq - x) % nx
    inner = jnp.where(cq == 0, dz * nx + dx, dx * nz + dz)
    index = jnp.where(cq == core, 0, chips) + inner
    ordered = stacked.at[index].get(mode="promise_in_bounds")
    ordered = jnp.transpose(ordered, (1, 0, 2, 3))
    return ordered.reshape(slots, rows, cols)


def shifted(value, step, groups):
    return lax.ppermute(value, "vgrp", [(g, (g + step) % groups) for g in range(groups)])


def prepare(total, vgrp, groups):
    pairs, rows, cols = total.shape
    block = rows // groups
    blocks = total.reshape(pairs, groups, block, cols)

    def pick(offset):
        return lax.dynamic_index_in_dim(blocks, (vgrp + offset) % groups, 1, keepdims=False)

    owed = tuple(pick(offset).astype(jnp.bfloat16) for offset in (1, -1, 2))
    return pick(0), owed


def exchange(own, owed, groups):
    ahead, behind, far = owed
    ahead = shifted(ahead, 1, groups)
    behind = shifted(behind, -1, groups)
    far = shifted(far, 2, groups)
    near = ahead.astype(jnp.float32) + behind.astype(jnp.float32)
    return own + near + far.astype(jnp.float32)


def columns(halves, vectors, lo, hi):
    total = None
    for slot, half_product in enumerate(halves):
        term = jnp.einsum(
            "pad,bd->pab", half_product, vectors[slot, lo:hi], preferred_element_type=jnp.float32
        )
        total = term if total is None else total + term
    return total


def on_device(amplitudes, cholesky_vectors, owner_order, sizes):
    vgrp = lax.axis_index("vgrp")
    groups = lax.psum(1, "vgrp")
    owned_slots = lax.dynamic_index_in_dim(owner_order, vgrp, 0, keepdims=False)
    vectors = gather_slots(cholesky_vectors[0, 0], owned_slots, sizes)
    halves = tuple(
        jnp.einsum(
            "ac,pcd->pad", vectors[slot], amplitudes, preferred_element_type=jnp.float32
        ).astype(jnp.bfloat16)
        for slot in range(vectors.shape[0])
    )
    split = vectors.shape[1] // 2
    own_a, owed_a = prepare(columns(halves, vectors, 0, split), vgrp, groups)
    halves, owed_a = lax.optimization_barrier((halves, owed_a))
    out_a = exchange(own_a, owed_a, groups)
    own_b, owed_b = prepare(columns(halves, vectors, split, None), vgrp, groups)
    out_b = exchange(own_b, owed_b, groups)
    return jnp.concatenate([out_a, out_b], axis=2)


def solution(mesh):
    pair, vgrp = mesh.devices.shape
    cores = 2
    chips = pair // cores
    side = RING
    assert chips == side * side
    devices = mesh.devices.reshape(chips // side, side, cores, vgrp)
    fine = Mesh(devices, ("z", "x", "core", "vgrp"))
    sizes = (chips // side, side, cores)
    placed = (P(PAIR, None, None), P("vgrp", PAIR, None, None), P())

    def body(amplitudes, cholesky_vectors, owner_order):
        return on_device(amplitudes, cholesky_vectors, owner_order, sizes)

    return jax.shard_map(
        body, mesh=fine, in_specs=placed, out_specs=P(PAIR, "vgrp", None), check_vma=False
    )
```

```python
import jax
import jax.numpy as jnp
from jax import lax
from jax.sharding import Mesh
from jax.sharding import PartitionSpec as P


PAIR = ("z", "x", "core")


RING = 4
CHUNKS = 6


def ring_axis(stage, core):
    return "x" if (stage == 1) == (core == 0) else "z"


def ring_perm(sizes, stage, step):
    nz, nx, nc = sizes
    perm = []
    for z in range(nz):
        for x in range(nx):
            for c in range(nc):
                if ring_axis(stage, c) == "x":
                    dz, dx = z, (x + step) % nx
                else:
                    dz, dx = (z + step) % nz, x
                perm.append(((z * nx + x) * nc + c, (dz * nx + dx) * nc + c))
    return perm


def ring_gather(piece, sizes, stage, direct_far=False):
    half = piece.shape[0] // 2
    from_prev = lax.ppermute(piece, PAIR, ring_perm(sizes, stage, 1))
    from_next = lax.ppermute(piece, PAIR, ring_perm(sizes, stage, -1))
    if direct_far:
        far = lax.ppermute(piece, PAIR, ring_perm(sizes, stage, 2))
    else:
        far_low = lax.ppermute(from_prev[:half], PAIR, ring_perm(sizes, stage, 1))
        far_high = lax.ppermute(from_next[half:], PAIR, ring_perm(sizes, stage, -1))
        far = jnp.concatenate([far_low, far_high], axis=0)
    return jnp.stack([piece, from_next, far, from_prev], axis=0)


def gather_slots(own_vector, owned_slots, sizes):
    nz, nx, nc = sizes
    rows, cols = own_vector.shape
    devices = nz * nx * nc
    piece = rows // devices
    slots = owned_slots.shape[0]
    pieces = own_vector.reshape(devices, piece, cols)
    pieces = lax.all_to_all(pieces, PAIR, 0, 0, tiled=True)
    picked = pieces.at[owned_slots].get(mode="promise_in_bounds")
    first = ring_gather(picked, sizes, 1, direct_far=True)
    both = ring_gather(first, sizes, 2)
    swap = [(q, q ^ 1) for q in range(devices)]
    other = lax.ppermute(both, PAIR, swap)
    chips = nz * nx
    stacked = jnp.concatenate(
        [both.reshape((chips,) + both.shape[2:]), other.reshape((chips,) + both.shape[2:])], axis=0
    )
    z = lax.axis_index("z")
    x = lax.axis_index("x")
    core = lax.axis_index("core")
    q = jnp.arange(devices, dtype=jnp.int32)
    zq, xq, cq = q // (nx * nc), (q // nc) % nx, q % nc
    dz, dx = (zq - z) % nz, (xq - x) % nx
    inner = jnp.where(cq == 0, dz * nx + dx, dx * nz + dz)
    index = jnp.where(cq == core, 0, chips) + inner
    ordered = stacked.at[index].get(mode="promise_in_bounds")
    ordered = jnp.transpose(ordered, (1, 0, 2, 3))
    return ordered.reshape(slots, rows, cols)


def shifted(value, step, groups):
    return lax.ppermute(value, "vgrp", [(g, (g + step) % groups) for g in range(groups)])


def prepare(total, vgrp, groups):
    pairs, rows, cols = total.shape
    block = rows // groups
    blocks = total.reshape(pairs, groups, block, cols)

    def pick(offset):
        return lax.dynamic_index_in_dim(blocks, (vgrp + offset) % groups, 1, keepdims=False)

    owed = tuple(pick(offset).astype(jnp.bfloat16) for offset in (1, -1, 2))
    return pick(0), owed


def exchange(own, owed, groups):
    ahead, behind, far = owed
    ahead = shifted(ahead, 1, groups)
    behind = shifted(behind, -1, groups)
    far = shifted(far, 2, groups)
    near = ahead.astype(jnp.float32) + behind.astype(jnp.float32)
    return own + near + far.astype(jnp.float32)


def columns(halves, vectors, lo, hi):
    total = None
    for slot, half_product in enumerate(halves):
        term = jnp.einsum(
            "pad,bd->pab", half_product, vectors[slot, lo:hi], preferred_element_type=jnp.float32
        )
        total = term if total is None else total + term
    return total


def on_device(amplitudes, cholesky_vectors, owner_order, sizes):
    vgrp = lax.axis_index("vgrp")
    groups = lax.psum(1, "vgrp")
    owned_slots = lax.dynamic_index_in_dim(owner_order, vgrp, 0, keepdims=False)
    vectors = gather_slots(cholesky_vectors[0, 0], owned_slots, sizes)
    halves = tuple(
        jnp.einsum(
            "ac,pcd->pad", vectors[slot], amplitudes, preferred_element_type=jnp.float32
        ).astype(jnp.bfloat16)
        for slot in range(vectors.shape[0])
    )
    width = vectors.shape[1] // CHUNKS
    outs = []
    for chunk in range(CHUNKS):
        cut = columns(halves, vectors, chunk * width, (chunk + 1) * width)
        own, owed = prepare(cut, vgrp, groups)
        if chunk < CHUNKS - 1:
            halves, owed = lax.optimization_barrier((halves, owed))
        outs.append(exchange(own, owed, groups))
    return jnp.concatenate(outs, axis=2)


def solution(mesh):
    pair, vgrp = mesh.devices.shape
    cores = 2
    chips = pair // cores
    side = RING
    assert chips == side * side
    devices = mesh.devices.reshape(chips // side, side, cores, vgrp)
    fine = Mesh(devices, ("z", "x", "core", "vgrp"))
    sizes = (chips // side, side, cores)
    placed = (P(PAIR, None, None), P("vgrp", PAIR, None, None), P())

    def body(amplitudes, cholesky_vectors, owner_order):
        return on_device(amplitudes, cholesky_vectors, owner_order, sizes)

    return jax.shard_map(
        body, mesh=fine, in_specs=placed, out_specs=P(PAIR, "vgrp", None), check_vma=False
    )
```

```python
import jax
import jax.numpy as jnp
from jax import lax
from jax.sharding import Mesh
from jax.sharding import PartitionSpec as P


PAIR = ("z", "x", "core")


RING = 4
CHUNKS = 3


def ring_axis(stage, core):
    return "x" if (stage == 1) == (core == 0) else "z"


def ring_perm(sizes, stage, step):
    nz, nx, nc = sizes
    perm = []
    for z in range(nz):
        for x in range(nx):
            for c in range(nc):
                if ring_axis(stage, c) == "x":
                    dz, dx = z, (x + step) % nx
                else:
                    dz, dx = (z + step) % nz, x
                perm.append(((z * nx + x) * nc + c, (dz * nx + dx) * nc + c))
    return perm


def ring_gather(piece, sizes, stage, direct_far=False):
    half = piece.shape[0] // 2
    from_prev = lax.ppermute(piece, PAIR, ring_perm(sizes, stage, 1))
    from_next = lax.ppermute(piece, PAIR, ring_perm(sizes, stage, -1))
    if direct_far:
        far = lax.ppermute(piece, PAIR, ring_perm(sizes, stage, 2))
    else:
        far_low = lax.ppermute(from_prev[:half], PAIR, ring_perm(sizes, stage, 1))
        far_high = lax.ppermute(from_next[half:], PAIR, ring_perm(sizes, stage, -1))
        far = jnp.concatenate([far_low, far_high], axis=0)
    return jnp.stack([piece, from_next, far, from_prev], axis=0)


def gather_slots(own_vector, owned_slots, sizes):
    nz, nx, nc = sizes
    rows, cols = own_vector.shape
    devices = nz * nx * nc
    piece = rows // devices
    slots = owned_slots.shape[0]
    pieces = own_vector.reshape(devices, piece, cols)
    pieces = lax.all_to_all(pieces, PAIR, 0, 0, tiled=True)
    picked = pieces.at[owned_slots].get(mode="promise_in_bounds")
    first = ring_gather(picked, sizes, 1, direct_far=True)
    both = ring_gather(first, sizes, 2)
    swap = [(q, q ^ 1) for q in range(devices)]
    other = lax.ppermute(both, PAIR, swap)
    chips = nz * nx
    stacked = jnp.concatenate(
        [both.reshape((chips,) + both.shape[2:]), other.reshape((chips,) + both.shape[2:])], axis=0
    )
    z = lax.axis_index("z")
    x = lax.axis_index("x")
    core = lax.axis_index("core")
    q = jnp.arange(devices, dtype=jnp.int32)
    zq, xq, cq = q // (nx * nc), (q // nc) % nx, q % nc
    dz, dx = (zq - z) % nz, (xq - x) % nx
    inner = jnp.where(cq == 0, dz * nx + dx, dx * nz + dz)
    index = jnp.where(cq == core, 0, chips) + inner
    ordered = stacked.at[index].get(mode="promise_in_bounds")
    ordered = jnp.transpose(ordered, (1, 0, 2, 3))
    return ordered.reshape(slots, rows, cols)


def shifted(value, step, groups):
    return lax.ppermute(value, "vgrp", [(g, (g + step) % groups) for g in range(groups)])


def prepare(total, vgrp, groups):
    pairs, rows, cols = total.shape
    block = rows // groups
    blocks = total.reshape(pairs, groups, block, cols)

    def pick(offset):
        return lax.dynamic_index_in_dim(blocks, (vgrp + offset) % groups, 1, keepdims=False)

    return pick(0), (pick(1), pick(-1), pick(2).astype(jnp.bfloat16))


def exchange(own, owed, groups):
    ahead, behind, far = owed
    half = far.shape[1] // 2
    far_up = shifted(far[:, :half], 1, groups)
    far_down = shifted(far[:, half:], -1, groups)
    ahead = jnp.concatenate([ahead[:, :half] + far_up.astype(jnp.float32), ahead[:, half:]], axis=1)
    behind = jnp.concatenate([behind[:, :half], behind[:, half:] + far_down.astype(jnp.float32)], axis=1)
    ahead = shifted(ahead.astype(jnp.bfloat16), 1, groups)
    behind = shifted(behind.astype(jnp.bfloat16), -1, groups)
    return own + ahead.astype(jnp.float32) + behind.astype(jnp.float32)


def columns(halves, vectors, lo, hi):
    total = None
    for slot, half_product in enumerate(halves):
        term = jnp.einsum(
            "pad,bd->pab", half_product, vectors[slot, lo:hi], preferred_element_type=jnp.float32
        )
        total = term if total is None else total + term
    return total


def on_device(amplitudes, cholesky_vectors, owner_order, sizes):
    vgrp = lax.axis_index("vgrp")
    groups = lax.psum(1, "vgrp")
    owned_slots = lax.dynamic_index_in_dim(owner_order, vgrp, 0, keepdims=False)
    vectors = gather_slots(cholesky_vectors[0, 0], owned_slots, sizes)
    halves = tuple(
        jnp.einsum(
            "ac,pcd->pad", vectors[slot], amplitudes, preferred_element_type=jnp.float32
        ).astype(jnp.bfloat16)
        for slot in range(vectors.shape[0])
    )
    width = vectors.shape[1] // CHUNKS
    outs = []
    for chunk in range(CHUNKS):
        cut = columns(halves, vectors, chunk * width, (chunk + 1) * width)
        own, owed = prepare(cut, vgrp, groups)
        if chunk < CHUNKS - 1:
            halves, owed = lax.optimization_barrier((halves, owed))
        outs.append(exchange(own, owed, groups))
    return jnp.concatenate(outs, axis=2)


def solution(mesh):
    pair, vgrp = mesh.devices.shape
    cores = 2
    chips = pair // cores
    side = RING
    assert chips == side * side
    devices = mesh.devices.reshape(chips // side, side, cores, vgrp)
    fine = Mesh(devices, ("z", "x", "core", "vgrp"))
    sizes = (chips // side, side, cores)
    placed = (P(PAIR, None, None), P("vgrp", PAIR, None, None), P())

    def body(amplitudes, cholesky_vectors, owner_order):
        return on_device(amplitudes, cholesky_vectors, owner_order, sizes)

    return jax.shard_map(
        body, mesh=fine, in_specs=placed, out_specs=P(PAIR, "vgrp", None), check_vma=False
    )
```

```python
import jax
import jax.numpy as jnp
from jax import lax
from jax.sharding import Mesh
from jax.sharding import PartitionSpec as P


PAIR = ("z", "x", "core")


RING = 4
CHUNKS = 3


def ring_axis(stage, core):
    return "x" if (stage == 1) == (core == 0) else "z"


def ring_perm(sizes, stage, step):
    nz, nx, nc = sizes
    perm = []
    for z in range(nz):
        for x in range(nx):
            for c in range(nc):
                if ring_axis(stage, c) == "x":
                    dz, dx = z, (x + step) % nx
                else:
                    dz, dx = (z + step) % nz, x
                perm.append(((z * nx + x) * nc + c, (dz * nx + dx) * nc + c))
    return perm


def ring_gather(piece, sizes, stage, direct_far=False):
    half = piece.shape[0] // 2
    from_prev = lax.ppermute(piece, PAIR, ring_perm(sizes, stage, 1))
    from_next = lax.ppermute(piece, PAIR, ring_perm(sizes, stage, -1))
    if direct_far:
        far = lax.ppermute(piece, PAIR, ring_perm(sizes, stage, 2))
    else:
        far_low = lax.ppermute(from_prev[:half], PAIR, ring_perm(sizes, stage, 1))
        far_high = lax.ppermute(from_next[half:], PAIR, ring_perm(sizes, stage, -1))
        far = jnp.concatenate([far_low, far_high], axis=0)
    return jnp.stack([piece, from_next, far, from_prev], axis=0)


def gather_slots(own_vector, owned_slots, sizes):
    nz, nx, nc = sizes
    rows, cols = own_vector.shape
    devices = nz * nx * nc
    piece = rows // devices
    slots = owned_slots.shape[0]
    pieces = own_vector.reshape(devices, piece, cols)
    pieces = lax.all_to_all(pieces, PAIR, 0, 0, tiled=True)
    picked = pieces.at[owned_slots].get(mode="promise_in_bounds")
    first = ring_gather(picked, sizes, 1, direct_far=True)
    both = ring_gather(first, sizes, 2)
    swap = [(q, q ^ 1) for q in range(devices)]
    other = lax.ppermute(both, PAIR, swap)
    chips = nz * nx
    stacked = jnp.concatenate(
        [both.reshape((chips,) + both.shape[2:]), other.reshape((chips,) + both.shape[2:])], axis=0
    )
    z = lax.axis_index("z")
    x = lax.axis_index("x")
    core = lax.axis_index("core")
    q = jnp.arange(devices, dtype=jnp.int32)
    zq, xq, cq = q // (nx * nc), (q // nc) % nx, q % nc
    dz, dx = (zq - z) % nz, (xq - x) % nx
    inner = jnp.where(cq == 0, dz * nx + dx, dx * nz + dz)
    index = jnp.where(cq == core, 0, chips) + inner
    return tuple(
        stacked[:, slot].at[index].get(mode="promise_in_bounds").reshape(rows, cols)
        for slot in range(slots)
    )


def shifted(value, step, groups):
    return lax.ppermute(value, "vgrp", [(g, (g + step) % groups) for g in range(groups)])


def prepare(total, vgrp, groups):
    pairs, rows, cols = total.shape
    block = rows // groups
    blocks = total.reshape(pairs, groups, block, cols)

    def pick(offset):
        return lax.dynamic_index_in_dim(blocks, (vgrp + offset) % groups, 1, keepdims=False)

    owed = tuple(pick(offset).astype(jnp.bfloat16) for offset in (1, -1, 2))
    return pick(0), owed


def exchange(own, owed, groups):
    ahead, behind, far = owed
    ahead = shifted(ahead, 1, groups)
    behind = shifted(behind, -1, groups)
    far = shifted(far, 2, groups)
    near = ahead.astype(jnp.float32) + behind.astype(jnp.float32)
    return own + near + far.astype(jnp.float32)


def columns(halves, vectors, lo, hi):
    total = None
    for slot, half_product in enumerate(halves):
        term = jnp.einsum(
            "pad,bd->pab", half_product, vectors[slot][lo:hi], preferred_element_type=jnp.float32
        )
        total = term if total is None else total + term
    return total


def on_device(amplitudes, cholesky_vectors, owner_order, sizes):
    vgrp = lax.axis_index("vgrp")
    groups = lax.psum(1, "vgrp")
    owned_slots = lax.dynamic_index_in_dim(owner_order, vgrp, 0, keepdims=False)
    vectors = gather_slots(cholesky_vectors[0, 0], owned_slots, sizes)
    halves = tuple(
        jnp.einsum(
            "ac,pcd->pad", vector, amplitudes, preferred_element_type=jnp.float32
        ).astype(jnp.bfloat16)
        for vector in vectors
    )
    width = vectors[0].shape[0] // CHUNKS
    outs = []
    for chunk in range(CHUNKS):
        cut = columns(halves, vectors, chunk * width, (chunk + 1) * width)
        own, owed = prepare(cut, vgrp, groups)
        if chunk < CHUNKS - 1:
            halves, owed = lax.optimization_barrier((halves, owed))
        outs.append(exchange(own, owed, groups))
    return jnp.concatenate(outs, axis=2)


def solution(mesh):
    pair, vgrp = mesh.devices.shape
    cores = 2
    chips = pair // cores
    side = RING
    assert chips == side * side
    devices = mesh.devices.reshape(chips // side, side, cores, vgrp)
    fine = Mesh(devices, ("z", "x", "core", "vgrp"))
    sizes = (chips // side, side, cores)
    placed = (P(PAIR, None, None), P("vgrp", PAIR, None, None), P())

    def body(amplitudes, cholesky_vectors, owner_order):
        return on_device(amplitudes, cholesky_vectors, owner_order, sizes)

    return jax.shard_map(
        body, mesh=fine, in_specs=placed, out_specs=P(PAIR, "vgrp", None), check_vma=False
    )
```

```python
import jax
import jax.numpy as jnp
from jax import lax
from jax.sharding import Mesh
from jax.sharding import PartitionSpec as P


PAIR = ("z", "x", "core")


RING = 4
CHUNKS = (1, 2, 3)


def ring_axis(stage, core):
    return "x" if (stage == 1) == (core == 0) else "z"


def ring_perm(sizes, stage, step):
    nz, nx, nc = sizes
    perm = []
    for z in range(nz):
        for x in range(nx):
            for c in range(nc):
                if ring_axis(stage, c) == "x":
                    dz, dx = z, (x + step) % nx
                else:
                    dz, dx = (z + step) % nz, x
                perm.append(((z * nx + x) * nc + c, (dz * nx + dx) * nc + c))
    return perm


def ring_gather(piece, sizes, stage, direct_far=False):
    half = piece.shape[0] // 2
    from_prev = lax.ppermute(piece, PAIR, ring_perm(sizes, stage, 1))
    from_next = lax.ppermute(piece, PAIR, ring_perm(sizes, stage, -1))
    if direct_far:
        far = lax.ppermute(piece, PAIR, ring_perm(sizes, stage, 2))
    else:
        far_low = lax.ppermute(from_prev[:half], PAIR, ring_perm(sizes, stage, 1))
        far_high = lax.ppermute(from_next[half:], PAIR, ring_perm(sizes, stage, -1))
        far = jnp.concatenate([far_low, far_high], axis=0)
    return jnp.stack([piece, from_next, far, from_prev], axis=0)


def gather_slots(own_vector, owned_slots, sizes):
    nz, nx, nc = sizes
    rows, cols = own_vector.shape
    devices = nz * nx * nc
    piece = rows // devices
    slots = owned_slots.shape[0]
    pieces = own_vector.reshape(devices, piece, cols)
    pieces = lax.all_to_all(pieces, PAIR, 0, 0, tiled=True)
    picked = pieces.at[owned_slots].get(mode="promise_in_bounds")
    first = ring_gather(picked, sizes, 1, direct_far=True)
    both = ring_gather(first, sizes, 2)
    swap = [(q, q ^ 1) for q in range(devices)]
    other = lax.ppermute(both, PAIR, swap)
    chips = nz * nx
    stacked = jnp.concatenate(
        [both.reshape((chips,) + both.shape[2:]), other.reshape((chips,) + both.shape[2:])], axis=0
    )
    z = lax.axis_index("z")
    x = lax.axis_index("x")
    core = lax.axis_index("core")
    q = jnp.arange(devices, dtype=jnp.int32)
    zq, xq, cq = q // (nx * nc), (q // nc) % nx, q % nc
    dz, dx = (zq - z) % nz, (xq - x) % nx
    inner = jnp.where(cq == 0, dz * nx + dx, dx * nz + dz)
    index = jnp.where(cq == core, 0, chips) + inner
    ordered = stacked.at[index].get(mode="promise_in_bounds")
    ordered = jnp.transpose(ordered, (1, 0, 2, 3))
    return ordered.reshape(slots, rows, cols)


def shifted(value, step, groups):
    return lax.ppermute(value, "vgrp", [(g, (g + step) % groups) for g in range(groups)])


def prepare(total, vgrp, groups):
    pairs, rows, cols = total.shape
    block = rows // groups
    blocks = total.reshape(pairs, groups, block, cols)

    def pick(offset):
        return lax.dynamic_index_in_dim(blocks, (vgrp + offset) % groups, 1, keepdims=False)

    owed = tuple(pick(offset).astype(jnp.bfloat16) for offset in (1, -1, 2))
    return pick(0), owed


def exchange(own, owed, groups):
    ahead, behind, far = owed
    ahead = shifted(ahead, 1, groups)
    behind = shifted(behind, -1, groups)
    far = shifted(far, 2, groups)
    near = ahead.astype(jnp.float32) + behind.astype(jnp.float32)
    return own + near + far.astype(jnp.float32)


def columns(halves, vectors, lo, hi):
    total = None
    for slot, half_product in enumerate(halves):
        term = jnp.einsum(
            "pad,bd->pab", half_product, vectors[slot, lo:hi], preferred_element_type=jnp.float32
        )
        total = term if total is None else total + term
    return total


def on_device(amplitudes, cholesky_vectors, owner_order, sizes):
    vgrp = lax.axis_index("vgrp")
    groups = lax.psum(1, "vgrp")
    owned_slots = lax.dynamic_index_in_dim(owner_order, vgrp, 0, keepdims=False)
    vectors = gather_slots(cholesky_vectors[0, 0], owned_slots, sizes)
    halves = tuple(
        jnp.einsum(
            "ac,pcd->pad", vectors[slot], amplitudes, preferred_element_type=jnp.float32
        ).astype(jnp.bfloat16)
        for slot in range(vectors.shape[0])
    )
    unit = vectors.shape[1] // sum(CHUNKS)
    edges = [0]
    for share in CHUNKS:
        edges.append(edges[-1] + share * unit)
    outs = []
    for chunk in range(len(CHUNKS)):
        cut = columns(halves, vectors, edges[chunk], edges[chunk + 1])
        own, owed = prepare(cut, vgrp, groups)
        if chunk < len(CHUNKS) - 1:
            halves, owed = lax.optimization_barrier((halves, owed))
        outs.append(exchange(own, owed, groups))
    return jnp.concatenate(outs, axis=2)


def solution(mesh):
    pair, vgrp = mesh.devices.shape
    cores = 2
    chips = pair // cores
    side = RING
    assert chips == side * side
    devices = mesh.devices.reshape(chips // side, side, cores, vgrp)
    fine = Mesh(devices, ("z", "x", "core", "vgrp"))
    sizes = (chips // side, side, cores)
    placed = (P(PAIR, None, None), P("vgrp", PAIR, None, None), P())

    def body(amplitudes, cholesky_vectors, owner_order):
        return on_device(amplitudes, cholesky_vectors, owner_order, sizes)

    return jax.shard_map(
        body, mesh=fine, in_specs=placed, out_specs=P(PAIR, "vgrp", None), check_vma=False
    )
```

```python
import jax
import jax.numpy as jnp
from jax import lax
from jax.sharding import Mesh
from jax.sharding import PartitionSpec as P


PAIR = ("z", "x", "core")


RING = 4
CHUNKS = 3


def ring_axis(stage, core):
    return "x" if (stage == 1) == (core == 0) else "z"


def ring_perm(sizes, stage, step):
    nz, nx, nc = sizes
    perm = []
    for z in range(nz):
        for x in range(nx):
            for c in range(nc):
                if ring_axis(stage, c) == "x":
                    dz, dx = z, (x + step) % nx
                else:
                    dz, dx = (z + step) % nz, x
                perm.append(((z * nx + x) * nc + c, (dz * nx + dx) * nc + c))
    return perm


def ring_gather(piece, sizes, stage, direct_far=False):
    half = piece.shape[0] // 2
    from_prev = lax.ppermute(piece, PAIR, ring_perm(sizes, stage, 1))
    from_next = lax.ppermute(piece, PAIR, ring_perm(sizes, stage, -1))
    if direct_far:
        far = lax.ppermute(piece, PAIR, ring_perm(sizes, stage, 2))
    else:
        far_low = lax.ppermute(from_prev[:half], PAIR, ring_perm(sizes, stage, 1))
        far_high = lax.ppermute(from_next[half:], PAIR, ring_perm(sizes, stage, -1))
        far = jnp.concatenate([far_low, far_high], axis=0)
    return jnp.stack([piece, from_next, far, from_prev], axis=0)


def gather_slots(own_vector, owned_slots, sizes):
    nz, nx, nc = sizes
    rows, cols = own_vector.shape
    devices = nz * nx * nc
    piece = rows // devices
    slots = owned_slots.shape[0]
    pieces = own_vector.reshape(devices, piece, cols)
    pieces = lax.all_to_all(pieces, PAIR, 0, 0, tiled=True)
    picked = pieces.at[owned_slots].get(mode="promise_in_bounds")
    first = ring_gather(picked, sizes, 1, direct_far=True)
    both = ring_gather(first, sizes, 2)
    chips = nz * nx
    stacked = lax.all_gather(both, "core", axis=0, tiled=False)
    stacked = stacked.reshape((nc * chips,) + both.shape[2:])
    z = lax.axis_index("z")
    x = lax.axis_index("x")
    q = jnp.arange(devices, dtype=jnp.int32)
    zq, xq, cq = q // (nx * nc), (q // nc) % nx, q % nc
    dz, dx = (zq - z) % nz, (xq - x) % nx
    inner = jnp.where(cq == 0, dz * nx + dx, dx * nz + dz)
    index = cq * chips + inner
    ordered = stacked.at[index].get(mode="promise_in_bounds")
    ordered = jnp.transpose(ordered, (1, 0, 2, 3))
    return ordered.reshape(slots, rows, cols)


def shifted(value, step, groups):
    return lax.ppermute(value, "vgrp", [(g, (g + step) % groups) for g in range(groups)])


def prepare(total, vgrp, groups):
    pairs, rows, cols = total.shape
    block = rows // groups
    blocks = total.reshape(pairs, groups, block, cols)

    def pick(offset):
        return lax.dynamic_index_in_dim(blocks, (vgrp + offset) % groups, 1, keepdims=False)

    owed = tuple(pick(offset).astype(jnp.bfloat16) for offset in (1, -1, 2))
    return pick(0), owed


def exchange(own, owed, groups):
    ahead, behind, far = owed
    ahead = shifted(ahead, 1, groups)
    behind = shifted(behind, -1, groups)
    far = shifted(far, 2, groups)
    near = ahead.astype(jnp.float32) + behind.astype(jnp.float32)
    return own + near + far.astype(jnp.float32)


def columns(halves, vectors, lo, hi):
    total = None
    for slot, half_product in enumerate(halves):
        term = jnp.einsum(
            "pad,bd->pab", half_product, vectors[slot, lo:hi], preferred_element_type=jnp.float32
        )
        total = term if total is None else total + term
    return total


def on_device(amplitudes, cholesky_vectors, owner_order, sizes):
    vgrp = lax.axis_index("vgrp")
    groups = lax.psum(1, "vgrp")
    owned_slots = lax.dynamic_index_in_dim(owner_order, vgrp, 0, keepdims=False)
    vectors = gather_slots(cholesky_vectors[0, 0], owned_slots, sizes)
    halves = tuple(
        jnp.einsum(
            "ac,pcd->pad", vectors[slot], amplitudes, preferred_element_type=jnp.float32
        ).astype(jnp.bfloat16)
        for slot in range(vectors.shape[0])
    )
    width = vectors.shape[1] // CHUNKS
    outs = []
    for chunk in range(CHUNKS):
        cut = columns(halves, vectors, chunk * width, (chunk + 1) * width)
        own, owed = prepare(cut, vgrp, groups)
        if chunk < CHUNKS - 1:
            halves, owed = lax.optimization_barrier((halves, owed))
        outs.append(exchange(own, owed, groups))
    return jnp.concatenate(outs, axis=2)


def solution(mesh):
    pair, vgrp = mesh.devices.shape
    cores = 2
    chips = pair // cores
    side = RING
    assert chips == side * side
    devices = mesh.devices.reshape(chips // side, side, cores, vgrp)
    fine = Mesh(devices, ("z", "x", "core", "vgrp"))
    sizes = (chips // side, side, cores)
    placed = (P(PAIR, None, None), P("vgrp", PAIR, None, None), P())

    def body(amplitudes, cholesky_vectors, owner_order):
        return on_device(amplitudes, cholesky_vectors, owner_order, sizes)

    return jax.shard_map(
        body, mesh=fine, in_specs=placed, out_specs=P(PAIR, "vgrp", None), check_vma=False
    )
```

```python
import jax
import jax.numpy as jnp
from jax import lax
from jax.sharding import Mesh
from jax.sharding import PartitionSpec as P


PAIR = ("z", "x", "core")


RING = 4
CHUNKS = 3


def ring_axis(stage, core):
    return "x" if (stage == 1) == (core == 0) else "z"


def ring_perm(sizes, stage, step):
    nz, nx, nc = sizes
    perm = []
    for z in range(nz):
        for x in range(nx):
            for c in range(nc):
                if ring_axis(stage, c) == "x":
                    dz, dx = z, (x + step) % nx
                else:
                    dz, dx = (z + step) % nz, x
                perm.append(((z * nx + x) * nc + c, (dz * nx + dx) * nc + c))
    return perm


def ring_gather(piece, sizes, stage, direct_far=False):
    half = piece.shape[0] // 2
    from_prev = lax.ppermute(piece, PAIR, ring_perm(sizes, stage, 1))
    from_next = lax.ppermute(piece, PAIR, ring_perm(sizes, stage, -1))
    if direct_far:
        far = lax.ppermute(piece, PAIR, ring_perm(sizes, stage, 2))
    else:
        far_low = lax.ppermute(from_prev[:half], PAIR, ring_perm(sizes, stage, 1))
        far_high = lax.ppermute(from_next[half:], PAIR, ring_perm(sizes, stage, -1))
        far = jnp.concatenate([far_low, far_high], axis=0)
    return [piece, from_next, far, from_prev]


def gather_slots(own_vector, owned_slots, sizes):
    nz, nx, nc = sizes
    rows, cols = own_vector.shape
    devices = nz * nx * nc
    piece = rows // devices
    slots = owned_slots.shape[0]
    pieces = own_vector.reshape(devices, piece, cols)
    pieces = lax.all_to_all(pieces, PAIR, 0, 0, tiled=True)
    picked = pieces.at[owned_slots].get(mode="promise_in_bounds")
    first = jnp.stack(ring_gather(picked, sizes, 1, direct_far=True), axis=0)
    both = ring_gather(first, sizes, 2)
    swap = [(q, q ^ 1) for q in range(devices)]
    other = [lax.ppermute(part, PAIR, swap) for part in both]
    chips = nz * nx
    stacked = jnp.concatenate(both + other, axis=0)
    z = lax.axis_index("z")
    x = lax.axis_index("x")
    core = lax.axis_index("core")
    q = jnp.arange(devices, dtype=jnp.int32)
    zq, xq, cq = q // (nx * nc), (q // nc) % nx, q % nc
    dz, dx = (zq - z) % nz, (xq - x) % nx
    inner = jnp.where(cq == 0, dz * nx + dx, dx * nz + dz)
    index = jnp.where(cq == core, 0, chips) + inner
    ordered = stacked.at[index].get(mode="promise_in_bounds")
    ordered = jnp.transpose(ordered, (1, 0, 2, 3))
    return ordered.reshape(slots, rows, cols)


def shifted(value, step, groups):
    return lax.ppermute(value, "vgrp", [(g, (g + step) % groups) for g in range(groups)])


def prepare(total, vgrp, groups):
    pairs, rows, cols = total.shape
    block = rows // groups
    blocks = total.reshape(pairs, groups, block, cols)

    def pick(offset):
        return lax.dynamic_index_in_dim(blocks, (vgrp + offset) % groups, 1, keepdims=False)

    owed = tuple(pick(offset).astype(jnp.bfloat16) for offset in (1, -1, 2))
    return pick(0), owed


def exchange(own, owed, groups):
    ahead, behind, far = owed
    ahead = shifted(ahead, 1, groups)
    behind = shifted(behind, -1, groups)
    far = shifted(far, 2, groups)
    near = ahead.astype(jnp.float32) + behind.astype(jnp.float32)
    return own + near + far.astype(jnp.float32)


def columns(halves, vectors, lo, hi):
    total = None
    for slot, half_product in enumerate(halves):
        term = jnp.einsum(
            "pad,bd->pab", half_product, vectors[slot, lo:hi], preferred_element_type=jnp.float32
        )
        total = term if total is None else total + term
    return total


def on_device(amplitudes, cholesky_vectors, owner_order, sizes):
    vgrp = lax.axis_index("vgrp")
    groups = lax.psum(1, "vgrp")
    owned_slots = lax.dynamic_index_in_dim(owner_order, vgrp, 0, keepdims=False)
    vectors = gather_slots(cholesky_vectors[0, 0], owned_slots, sizes)
    halves = tuple(
        jnp.einsum(
            "ac,pcd->pad", vectors[slot], amplitudes, preferred_element_type=jnp.float32
        ).astype(jnp.bfloat16)
        for slot in range(vectors.shape[0])
    )
    width = vectors.shape[1] // CHUNKS
    outs = []
    for chunk in range(CHUNKS):
        cut = columns(halves, vectors, chunk * width, (chunk + 1) * width)
        own, owed = prepare(cut, vgrp, groups)
        if chunk < CHUNKS - 1:
            halves, owed = lax.optimization_barrier((halves, owed))
        outs.append(exchange(own, owed, groups))
    return jnp.concatenate(outs, axis=2)


def solution(mesh):
    pair, vgrp = mesh.devices.shape
    cores = 2
    chips = pair // cores
    side = RING
    assert chips == side * side
    devices = mesh.devices.reshape(chips // side, side, cores, vgrp)
    fine = Mesh(devices, ("z", "x", "core", "vgrp"))
    sizes = (chips // side, side, cores)
    placed = (P(PAIR, None, None), P("vgrp", PAIR, None, None), P())

    def body(amplitudes, cholesky_vectors, owner_order):
        return on_device(amplitudes, cholesky_vectors, owner_order, sizes)

    return jax.shard_map(
        body, mesh=fine, in_specs=placed, out_specs=P(PAIR, "vgrp", None), check_vma=False
    )
```

```python
import jax
import jax.numpy as jnp
from jax import lax
from jax.sharding import Mesh
from jax.sharding import PartitionSpec as P


PAIR = ("z", "x", "core")


RING = 4
CHUNKS = 3


def ring_axis(stage, core):
    return "x" if (stage == 1) == (core == 0) else "z"


def ring_perm(sizes, stage, step):
    nz, nx, nc = sizes
    perm = []
    for z in range(nz):
        for x in range(nx):
            for c in range(nc):
                if ring_axis(stage, c) == "x":
                    dz, dx = z, (x + step) % nx
                else:
                    dz, dx = (z + step) % nz, x
                perm.append(((z * nx + x) * nc + c, (dz * nx + dx) * nc + c))
    return perm


def ring_gather(piece, sizes, stage, direct_far=False):
    half = piece.shape[0] // 2
    from_prev = lax.ppermute(piece, PAIR, ring_perm(sizes, stage, 1))
    from_next = lax.ppermute(piece, PAIR, ring_perm(sizes, stage, -1))
    if direct_far:
        far = lax.ppermute(piece, PAIR, ring_perm(sizes, stage, 2))
    else:
        far_low = lax.ppermute(from_prev[:half], PAIR, ring_perm(sizes, stage, 1))
        far_high = lax.ppermute(from_next[half:], PAIR, ring_perm(sizes, stage, -1))
        far = jnp.concatenate([far_low, far_high], axis=0)
    return [piece, from_next, far, from_prev]


def gather_slots(own_vector, owned_slots, sizes):
    nz, nx, nc = sizes
    rows, cols = own_vector.shape
    devices = nz * nx * nc
    piece = rows // devices
    slots = owned_slots.shape[0]
    pieces = own_vector.reshape(devices, piece, cols)
    pieces = lax.all_to_all(pieces, PAIR, 0, 0, tiled=True)
    picked = pieces.at[owned_slots].get(mode="promise_in_bounds")
    first = jnp.stack(ring_gather(picked, sizes, 1, direct_far=True), axis=0)
    both = ring_gather(first, sizes, 2)
    swap = [(q, q ^ 1) for q in range(devices)]
    other = [lax.ppermute(part, PAIR, swap) for part in both]
    z = lax.axis_index("z")
    x = lax.axis_index("x")
    core = lax.axis_index("core")
    ordered = jnp.zeros((slots, devices, piece, cols), own_vector.dtype)
    for c, parts in ((core, both), (1 - core, other)):
        for outer, part in enumerate(parts):
            for inner in range(part.shape[0]):
                dz = jnp.where(c == 0, outer, inner)
                dx = jnp.where(c == 0, inner, outer)
                q = (((z + dz) % nz) * nx + (x + dx) % nx) * nc + c
                ordered = lax.dynamic_update_slice(ordered, part[inner][:, None], (0, q, 0, 0))
    return ordered.reshape(slots, rows, cols)


def shifted(value, step, groups):
    return lax.ppermute(value, "vgrp", [(g, (g + step) % groups) for g in range(groups)])


def prepare(total, vgrp, groups):
    pairs, rows, cols = total.shape
    block = rows // groups
    blocks = total.reshape(pairs, groups, block, cols)

    def pick(offset):
        return lax.dynamic_index_in_dim(blocks, (vgrp + offset) % groups, 1, keepdims=False)

    owed = tuple(pick(offset).astype(jnp.bfloat16) for offset in (1, -1, 2))
    return pick(0), owed


def exchange(own, owed, groups):
    ahead, behind, far = owed
    ahead = shifted(ahead, 1, groups)
    behind = shifted(behind, -1, groups)
    far = shifted(far, 2, groups)
    near = ahead.astype(jnp.float32) + behind.astype(jnp.float32)
    return own + near + far.astype(jnp.float32)


def columns(halves, vectors, lo, hi):
    total = None
    for slot, half_product in enumerate(halves):
        term = jnp.einsum(
            "pad,bd->pab", half_product, vectors[slot, lo:hi], preferred_element_type=jnp.float32
        )
        total = term if total is None else total + term
    return total


def on_device(amplitudes, cholesky_vectors, owner_order, sizes):
    vgrp = lax.axis_index("vgrp")
    groups = lax.psum(1, "vgrp")
    owned_slots = lax.dynamic_index_in_dim(owner_order, vgrp, 0, keepdims=False)
    vectors = gather_slots(cholesky_vectors[0, 0], owned_slots, sizes)
    halves = tuple(
        jnp.einsum(
            "ac,pcd->pad", vectors[slot], amplitudes, preferred_element_type=jnp.float32
        ).astype(jnp.bfloat16)
        for slot in range(vectors.shape[0])
    )
    width = vectors.shape[1] // CHUNKS
    outs = []
    for chunk in range(CHUNKS):
        cut = columns(halves, vectors, chunk * width, (chunk + 1) * width)
        own, owed = prepare(cut, vgrp, groups)
        if chunk < CHUNKS - 1:
            halves, owed = lax.optimization_barrier((halves, owed))
        outs.append(exchange(own, owed, groups))
    return jnp.concatenate(outs, axis=2)


def solution(mesh):
    pair, vgrp = mesh.devices.shape
    cores = 2
    chips = pair // cores
    side = RING
    assert chips == side * side
    devices = mesh.devices.reshape(chips // side, side, cores, vgrp)
    fine = Mesh(devices, ("z", "x", "core", "vgrp"))
    sizes = (chips // side, side, cores)
    placed = (P(PAIR, None, None), P("vgrp", PAIR, None, None), P())

    def body(amplitudes, cholesky_vectors, owner_order):
        return on_device(amplitudes, cholesky_vectors, owner_order, sizes)

    return jax.shard_map(
        body, mesh=fine, in_specs=placed, out_specs=P(PAIR, "vgrp", None), check_vma=False
    )
```

```python
import jax
import jax.numpy as jnp
from jax import lax
from jax.sharding import Mesh
from jax.sharding import PartitionSpec as P


PAIR = ("z", "x", "core")


RING = 4
CHUNKS = 3


def ring_axis(stage, core):
    return "x" if (stage == 1) == (core == 0) else "z"


def ring_perm(sizes, stage, step):
    nz, nx, nc = sizes
    perm = []
    for z in range(nz):
        for x in range(nx):
            for c in range(nc):
                if ring_axis(stage, c) == "x":
                    dz, dx = z, (x + step) % nx
                else:
                    dz, dx = (z + step) % nz, x
                perm.append(((z * nx + x) * nc + c, (dz * nx + dx) * nc + c))
    return perm


def ring_gather(piece, sizes, stage, direct_far=False):
    half = piece.shape[0] // 2
    from_prev = lax.ppermute(piece, PAIR, ring_perm(sizes, stage, 1))
    from_next = lax.ppermute(piece, PAIR, ring_perm(sizes, stage, -1))
    if direct_far:
        far = lax.ppermute(piece, PAIR, ring_perm(sizes, stage, 2))
    else:
        far_low = lax.ppermute(from_prev[:half], PAIR, ring_perm(sizes, stage, 1))
        far_high = lax.ppermute(from_next[half:], PAIR, ring_perm(sizes, stage, -1))
        far = jnp.concatenate([far_low, far_high], axis=0)
    return [piece, from_next, far, from_prev]


def gather_slots(own_vector, owned_slots, sizes):
    nz, nx, nc = sizes
    rows, cols = own_vector.shape
    devices = nz * nx * nc
    piece = rows // devices
    slots = owned_slots.shape[0]
    pieces = own_vector.reshape(devices, piece, cols)
    pieces = lax.all_to_all(pieces, PAIR, 0, 0, tiled=True)
    picked = pieces.at[owned_slots].get(mode="promise_in_bounds")
    first = jnp.zeros((RING,) + picked.shape, picked.dtype)
    for offset, part in enumerate(ring_gather(picked, sizes, 1, direct_far=True)):
        first = lax.dynamic_update_slice(first, part[None], (offset, 0, 0, 0))
    both = ring_gather(first, sizes, 2)
    swap = [(q, q ^ 1) for q in range(devices)]
    other = [lax.ppermute(part, PAIR, swap) for part in both]
    z = lax.axis_index("z")
    x = lax.axis_index("x")
    core = lax.axis_index("core")
    ordered = jnp.zeros((slots, devices, piece, cols), own_vector.dtype)
    for c, parts in ((core, both), (1 - core, other)):
        for outer, part in enumerate(parts):
            for inner in range(part.shape[0]):
                dz = jnp.where(c == 0, outer, inner)
                dx = jnp.where(c == 0, inner, outer)
                q = (((z + dz) % nz) * nx + (x + dx) % nx) * nc + c
                ordered = lax.dynamic_update_slice(ordered, part[inner][:, None], (0, q, 0, 0))
    return ordered.reshape(slots, rows, cols)


def shifted(value, step, groups):
    return lax.ppermute(value, "vgrp", [(g, (g + step) % groups) for g in range(groups)])


def prepare(total, vgrp, groups):
    pairs, rows, cols = total.shape
    block = rows // groups
    blocks = total.reshape(pairs, groups, block, cols)

    def pick(offset):
        return lax.dynamic_index_in_dim(blocks, (vgrp + offset) % groups, 1, keepdims=False)

    owed = tuple(pick(offset).astype(jnp.bfloat16) for offset in (1, -1, 2))
    return pick(0), owed


def exchange(own, owed, groups):
    ahead, behind, far = owed
    ahead = shifted(ahead, 1, groups)
    behind = shifted(behind, -1, groups)
    far = shifted(far, 2, groups)
    near = ahead.astype(jnp.float32) + behind.astype(jnp.float32)
    return own + near + far.astype(jnp.float32)


def columns(halves, vectors, lo, hi):
    total = None
    for slot, half_product in enumerate(halves):
        term = jnp.einsum(
            "pad,bd->pab", half_product, vectors[slot, lo:hi], preferred_element_type=jnp.float32
        )
        total = term if total is None else total + term
    return total


def on_device(amplitudes, cholesky_vectors, owner_order, sizes):
    vgrp = lax.axis_index("vgrp")
    groups = lax.psum(1, "vgrp")
    owned_slots = lax.dynamic_index_in_dim(owner_order, vgrp, 0, keepdims=False)
    vectors = gather_slots(cholesky_vectors[0, 0], owned_slots, sizes)
    halves = tuple(
        jnp.einsum(
            "ac,pcd->pad", vectors[slot], amplitudes, preferred_element_type=jnp.float32
        ).astype(jnp.bfloat16)
        for slot in range(vectors.shape[0])
    )
    width = vectors.shape[1] // CHUNKS
    result = None
    for chunk in range(CHUNKS):
        cut = columns(halves, vectors, chunk * width, (chunk + 1) * width)
        own, owed = prepare(cut, vgrp, groups)
        if chunk < CHUNKS - 1:
            halves, owed = lax.optimization_barrier((halves, owed))
        part = exchange(own, owed, groups)
        if result is None:
            result = jnp.zeros(part.shape[:2] + (vectors.shape[1],), part.dtype)
        result = lax.dynamic_update_slice(result, part, (0, 0, chunk * width))
    return result


def solution(mesh):
    pair, vgrp = mesh.devices.shape
    cores = 2
    chips = pair // cores
    side = RING
    assert chips == side * side
    devices = mesh.devices.reshape(chips // side, side, cores, vgrp)
    fine = Mesh(devices, ("z", "x", "core", "vgrp"))
    sizes = (chips // side, side, cores)
    placed = (P(PAIR, None, None), P("vgrp", PAIR, None, None), P())

    def body(amplitudes, cholesky_vectors, owner_order):
        return on_device(amplitudes, cholesky_vectors, owner_order, sizes)

    return jax.shard_map(
        body, mesh=fine, in_specs=placed, out_specs=P(PAIR, "vgrp", None), check_vma=False
    )
```
